128 devices in a mesh: tm: 32 (over y_lo, z, x), rows: 4 (over y_hi, core).
Axes of the slice: x: 4, y: 4 (y_hi: 2, y_lo: 2; y = y_hi * 2 + y_lo), z: 4, core: 2. Of those that a mesh axis runs over, the one named last changes fastest.
Arguments:
- features: bfloat16 [128, 96, 16, 256], P('tm', None, 'rows'), may hold values from -6 to 6
- first_kernel: bfloat16 [3, 3, 3, 96, 96], replicated, may hold values from -0.125 to 0.125
- first_bias: float32 [96], replicated, may hold values from -3 to 3
- first_gain: float32 [96], replicated, may hold values from 0.1 to 1.9
- second_kernel: bfloat16 [3, 3, 3, 96, 96], replicated, may hold values from -0.125 to 0.125
- latent_weight: bfloat16 [4, 16, 96], replicated, may hold values from -0.3125 to 0.3125
- decode_kernel: bfloat16 [3, 3, 3, 96, 16], replicated, may hold values from -0.3125 to 0.3125
- decode_bias: float32 [96], replicated, may hold values from -3 to 3
- decode_gain: float32 [96], replicated, may hold values from 0.1 to 1.9
- upsample_weight: bfloat16 [4, 96, 96], replicated, may hold values from -0.625 to 0.625
- final_kernel: bfloat16 [3, 3, 3, 96, 96], replicated, may hold values from -0.125 to 0.125
Outputs:
- latents: bfloat16 [32, 16, 16, 256], P('tm', None, 'rows')
- rebuilt: bfloat16 [128, 96, 16, 256], P('tm', None, 'rows')
The draws below stay inside these ranges and needn't reach their ends.
All inputs are finite; a program needn't handle non-finite values.
Results may differ from the reference program's by a relative error of at most 0.01.
Values may be sent and summed in bfloat16 or wider, within the bound.
No kernel may reach another device: no remote copies, remote signals or barrier semaphores. Data moves between devices by JAX's collectives and lax.ppermute only.
A program may use at most 64 MiB of HBM per device.

```python
import jax
import jax.numpy as jnp
from jax import lax

C = 96
Z = 16
SPAN = 4
COLS = 256
FRAMES = 128
LATENTS = 32
ROWS = 16


def steps_of(own_key, shape, shards, least, top_value):
    loudness, own = 1.0, jax.random.fold_in(own_key, 6)
    for position, parts in shards:
        heights = jnp.exp(jax.random.uniform(jax.random.fold_in(own, position), (parts,), jnp.float32, least / len(shards), top_value / len(shards)))
        loudness = loudness * jnp.repeat(heights, shape[position] // parts).reshape([-1 if axis == position else 1 for axis in range(len(shape))])
    return loudness


def bell_draw(own_key, shape, width, reach, split=(), held_as=jnp.bfloat16):
    drawn = width * jax.random.normal(own_key, shape, jnp.float32)
    if split:
        drawn = drawn * steps_of(own_key, shape, split, -0.22, 0.18)
    return jnp.clip(drawn, -reach, reach).astype(held_as)


def setup_inputs(seed: int = 0) -> dict:
    seeds = jax.random.split(jax.random.key(seed), 12)
    return {
        "features": bell_draw(seeds[0], (FRAMES, C, ROWS, COLS), 1.0, 6.0, ((0, 32), (2, 4))),
        "first_kernel": bell_draw(seeds[1], (3, 3, 3, C, C), (27 * C) ** -0.5, 0.125),
        "first_bias": bell_draw(seeds[2], (C,), 0.5, 3.0, (), jnp.float32),
        "first_gain": jnp.clip(1.0 + 0.18 * jax.random.normal(seeds[3], (C,), jnp.float32), 0.1, 1.9),
        "second_kernel": bell_draw(seeds[4], (3, 3, 3, C, C), (27 * C) ** -0.5, 0.125),
        "latent_weight": bell_draw(seeds[5], (SPAN, Z, C), (SPAN * C) ** -0.5, 0.3125),
        "decode_kernel": bell_draw(seeds[6], (3, 3, 3, C, Z), (27 * Z) ** -0.5, 0.3125),
        "decode_bias": bell_draw(seeds[7], (C,), 0.5, 3.0, (), jnp.float32),
        "decode_gain": jnp.clip(1.0 + 0.18 * jax.random.normal(seeds[8], (C,), jnp.float32), 0.1, 1.9),
        "upsample_weight": bell_draw(seeds[9], (SPAN, C, C), C ** -0.5, 0.625),
        "final_kernel": bell_draw(seeds[10], (3, 3, 3, C, C), (27 * C) ** -0.5, 0.125),
    }


def causal_conv(values, kernel):
    left_side = values.astype(jnp.float32).transpose(1, 0, 2, 3)[None]
    right_side = kernel.astype(jnp.float32).transpose(3, 4, 0, 1, 2)
    result = lax.conv_general_dilated(left_side, right_side, (1, 1, 1), [(2, 0), (1, 1), (1, 1)], dimension_numbers=('NCDHW', 'OIDHW', 'NCDHW'), precision=lax.Precision.HIGHEST)
    return result[0].transpose(1, 0, 2, 3)

def normed_silu(values, gain):
    scale = lax.rsqrt(lax.optimization_barrier(jnp.mean(values * values, axis=1, keepdims=True)) + 1e-06)
    return jax.nn.silu(values * scale * gain.astype(jnp.float32)[None, :, None, None])

def reference(features, first_kernel, first_bias, first_gain, second_kernel, latent_weight, decode_kernel, decode_bias, decode_gain, upsample_weight, final_kernel):
    first = causal_conv(features, first_kernel) + first_bias.astype(jnp.float32)[None, :, None, None]
    gated = normed_silu(first, first_gain).astype(jnp.bfloat16)
    hidden = (features.astype(jnp.float32) + causal_conv(gated, second_kernel)).astype(jnp.bfloat16)
    grouped = hidden.astype(jnp.float32).reshape(LATENTS, SPAN, C, ROWS, COLS)
    latents = jnp.einsum('jzc,kjcrw->kzrw', latent_weight.astype(jnp.float32), grouped, precision=lax.Precision.HIGHEST).astype(jnp.bfloat16)
    decoded = causal_conv(latents, decode_kernel) + decode_bias.astype(jnp.float32)[None, :, None, None]
    activated = normed_silu(decoded, decode_gain).astype(jnp.bfloat16)
    upsampled = jnp.einsum('joc,kcrw->kjorw', upsample_weight.astype(jnp.float32), activated.astype(jnp.float32), precision=lax.Precision.HIGHEST)
    upsampled = upsampled.reshape(FRAMES, C, ROWS, COLS).astype(jnp.bfloat16)
    rebuilt = (upsampled.astype(jnp.float32) + causal_conv(upsampled, final_kernel)).astype(jnp.bfloat16)
    return (latents, rebuilt)
```

```python
import jax
import jax.numpy as jnp
from jax import lax
from jax.sharding import PartitionSpec as P


def shift(x, dt, dr):
    nt = lax.axis_size("tm")
    nr = lax.axis_size("rows")
    if dt == 0:
        pairs = [(r, r + dr) for r in range(nr) if 0 <= r + dr < nr]
        return lax.ppermute(x, "rows", pairs)
    if dr == 0:
        pairs = [(t, t + dt) for t in range(nt) if 0 <= t + dt < nt]
        return lax.ppermute(x, "tm", pairs)
    pairs = [
        (t * nr + r, (t + dt) * nr + r + dr)
        for t in range(nt)
        for r in range(nr)
        if 0 <= t + dt < nt and 0 <= r + dr < nr
    ]
    return lax.ppermute(x, ("tm", "rows"), pairs)


def haloed_input(v):
    prev = shift(v[-2:], 1, 0)
    top = shift(v[:, :, -1:], 0, 1)
    bottom = shift(v[:, :, :1], 0, -1)
    top_corner = shift(v[-2:, :, -1:], 1, 1)
    bottom_corner = shift(v[-2:, :, :1], 1, -1)
    own = jnp.concatenate([top, v, bottom], 2)
    before = jnp.concatenate([top_corner, prev, bottom_corner], 2)
    return jnp.concatenate([before, own], 0)


def conv_valid(v, kernel):
    out = lax.conv_general_dilated(
        v[None],
        kernel,
        (1, 1, 1),
        [(0, 0), (0, 0), (1, 1)],
        dimension_numbers=("NDCHW", "DHWOI", "NDCHW"),
        preferred_element_type=jnp.float32,
    )
    return out[0]


def normed_silu(values, gain):
    scale = lax.rsqrt(jnp.mean(values * values, axis=1, keepdims=True) + 1e-06)
    return jax.nn.silu(values * scale * gain[None, :, None, None])


def body(
    features,
    first_kernel,
    first_bias,
    first_gain,
    second_kernel,
    latent_weight,
    decode_kernel,
    decode_bias,
    decode_gain,
    upsample_weight,
    final_kernel,
):
    channels = features.shape[1]
    band_rows = features.shape[2]
    columns = features.shape[3]
    span_len = features.shape[0]
    first = conv_valid(haloed_input(features), first_kernel) + first_bias[None, :, None, None]
    gated = normed_silu(first, first_gain).astype(jnp.bfloat16)
    hidden = (features.astype(jnp.float32) + conv_valid(haloed_input(gated), second_kernel)).astype(
        jnp.bfloat16
    )
    latent = jnp.einsum("jzc,jcrw->zrw", latent_weight, hidden, preferred_element_type=jnp.float32)[
        None
    ].astype(jnp.bfloat16)
    lat_rows = jnp.concatenate(
        [shift(latent[:, :, -2:], 0, 1), latent, shift(latent[:, :, :2], 0, -1)], 2
    )
    stacked = jnp.concatenate(
        [shift(lat_rows, 3, 0), shift(lat_rows, 2, 0), shift(lat_rows, 1, 0), lat_rows], 0
    )
    decoded = conv_valid(stacked, decode_kernel) + decode_bias[None, :, None, None]
    activated = normed_silu(decoded, decode_gain).astype(jnp.bfloat16)
    upsampled = jnp.einsum(
        "joc,kcrw->kjorw", upsample_weight, activated, preferred_element_type=jnp.float32
    )
    upsampled = upsampled.reshape(-1, channels, band_rows + 2, columns).astype(jnp.bfloat16)
    band = lax.axis_index("rows")
    bands = lax.axis_size("rows")
    row_ids = lax.broadcasted_iota(jnp.int32, (1, 1, band_rows + 2, 1), 2)
    inside = ((row_ids > 0) | (band > 0)) & ((row_ids < band_rows + 1) | (band < bands - 1))
    upsampled = jnp.where(inside, upsampled, jnp.zeros_like(upsampled))
    own_frames = upsampled[span_len:]
    previous = upsampled[span_len - 2 : span_len]
    previous = jnp.where(lax.axis_index("tm") > 0, previous, jnp.zeros_like(previous))
    branch = conv_valid(jnp.concatenate([previous, own_frames], 0), final_kernel)
    rebuilt = (own_frames[:, :, 1:-1].astype(jnp.float32) + branch).astype(jnp.bfloat16)
    return (latent, rebuilt)


def solution(mesh):
    return jax.shard_map(
        body,
        mesh=mesh,
        in_specs=(P("tm", None, "rows", None), P(), P(), P(), P(), P(), P(), P(), P(), P(), P()),
        out_specs=(P("tm", None, "rows", None), P("tm", None, "rows", None)),
        check_vma=False,
    )
```

```python
import functools

import jax
import jax.numpy as jnp
from jax import lax
from jax.experimental import pallas as pl
from jax.experimental.pallas import tpu as pltpu
from jax.sharding import PartitionSpec as P


def shift(x, dt, dr):
    nt = lax.axis_size("tm")
    nr = lax.axis_size("rows")
    if dt == 0:
        pairs = [(r, r + dr) for r in range(nr) if 0 <= r + dr < nr]
        return lax.ppermute(x, "rows", pairs)
    if dr == 0:
        pairs = [(t, t + dt) for t in range(nt) if 0 <= t + dt < nt]
        return lax.ppermute(x, "tm", pairs)
    pairs = [
        (t * nr + r, (t + dt) * nr + r + dr)
        for t in range(nt)
        for r in range(nr)
        if 0 <= t + dt < nt and 0 <= r + dr < nr
    ]
    return lax.ppermute(x, ("tm", "rows"), pairs)


def haloed_rows_first(v):
    prev = shift(v[-2:], 1, 0)
    top = shift(v[:, -1:], 0, 1)
    bottom = shift(v[:, :1], 0, -1)
    top_corner = shift(v[-2:, -1:], 1, 1)
    bottom_corner = shift(v[-2:, :1], 1, -1)
    own = jnp.concatenate([top, v, bottom], 1)
    before = jnp.concatenate([top_corner, prev, bottom_corner], 1)
    return jnp.concatenate([before, own], 0)


def merged_kernel(kernel):
    o, c = kernel.shape[3], kernel.shape[4]
    return kernel.transpose(2, 3, 0, 1, 4).reshape(3 * o, 9 * c)


def tap_sum(x_ref, k_ref, t, rows, columns):
    pieces = []
    for a in range(3):
        for b in range(3):
            pieces.append(
                jnp.concatenate([x_ref[t + a, r + b] for r in range(rows)], axis=1)
            )
    stacked = jnp.concatenate(pieces, axis=0)
    acc = jnp.dot(k_ref[...], stacked, preferred_element_type=jnp.float32)
    out_channels = acc.shape[0] // 3
    width = rows * columns
    lane = lax.broadcasted_iota(jnp.int32, (out_channels, width), 1) % columns
    left = pltpu.roll(acc[:out_channels], 1, 1)
    right = pltpu.roll(acc[2 * out_channels :], width - 1, 1)
    left = jnp.where(lane == 0, 0.0, left)
    right = jnp.where(lane == columns - 1, 0.0, right)
    return left + acc[out_channels : 2 * out_channels] + right


def gate_kernel(x_ref, k_ref, bias_ref, gain_ref, o_ref, *, frames, rows, columns):
    bias = bias_ref[...]
    gain = gain_ref[...]
    for t in range(frames):
        y = tap_sum(x_ref, k_ref, t, rows, columns) + bias
        scale = lax.rsqrt(jnp.mean(y * y, axis=0, keepdims=True) + 1e-06)
        z = y * scale * gain
        g = (z / (1.0 + jnp.exp(-z))).astype(o_ref.dtype)
        for r in range(rows):
            o_ref[t, r] = g[:, r * columns : (r + 1) * columns]


def latent_kernel(x_ref, k_ref, res_ref, w_ref, o_ref, *, frames, rows, columns):
    total = None
    for t in range(frames):
        y = tap_sum(x_ref, k_ref, t, rows, columns)
        res = jnp.concatenate([res_ref[t, r] for r in range(rows)], axis=1)
        hidden = (res.astype(jnp.float32) + y).astype(jnp.bfloat16)
        part = jnp.dot(w_ref[t], hidden, preferred_element_type=jnp.float32)
        total = part if total is None else total + part
    o_ref[...] = total.astype(o_ref.dtype)


def rebuild_kernel(x_ref, k_ref, o_ref, *, frames, rows, columns):
    for t in range(frames):
        y = tap_sum(x_ref, k_ref, t, rows, columns)
        res = jnp.concatenate([x_ref[t + 2, r + 1] for r in range(rows)], axis=1)
        o_ref[t] = (res.astype(jnp.float32) + y).astype(o_ref.dtype)


def normed_silu(values, gain):
    scale = lax.rsqrt(jnp.mean(values * values, axis=1, keepdims=True) + 1e-06)
    return jax.nn.silu(values * scale * gain[None, :, None, None])


def conv_valid(v, kernel):
    out = lax.conv_general_dilated(
        v[None],
        kernel,
        (1, 1, 1),
        [(0, 0), (0, 0), (1, 1)],
        dimension_numbers=("NDCHW", "DHWOI", "NDCHW"),
        preferred_element_type=jnp.float32,
    )
    return out[0]


def body(
    features,
    first_kernel,
    first_bias,
    first_gain,
    second_kernel,
    latent_weight,
    decode_kernel,
    decode_bias,
    decode_gain,
    upsample_weight,
    final_kernel,
):
    frames, channels, rows, columns = features.shape
    z_count = latent_weight.shape[1]
    dims = dict(frames=frames, rows=rows, columns=columns)
    own = features.transpose(0, 2, 1, 3)
    gated = pl.pallas_call(
        functools.partial(gate_kernel, **dims),
        out_shape=jax.ShapeDtypeStruct((frames, rows, channels, columns), jnp.bfloat16),
    )(
        haloed_rows_first(own),
        merged_kernel(first_kernel),
        first_bias[:, None],
        first_gain[:, None],
    )
    latent_flat = pl.pallas_call(
        functools.partial(latent_kernel, **dims),
        out_shape=jax.ShapeDtypeStruct((z_count, rows * columns), jnp.bfloat16),
    )(haloed_rows_first(gated), merged_kernel(second_kernel), own, latent_weight)
    latent = latent_flat.reshape(1, z_count, rows, columns)
    lat_rows = jnp.concatenate(
        [shift(latent[:, :, -2:], 0, 1), latent, shift(latent[:, :, :2], 0, -1)], 2
    )
    stacked = jnp.concatenate(
        [shift(lat_rows, 3, 0), shift(lat_rows, 2, 0), shift(lat_rows, 1, 0), lat_rows], 0
    )
    decoded = conv_valid(stacked, decode_kernel) + decode_bias[None, :, None, None]
    activated = normed_silu(decoded, decode_gain).astype(jnp.bfloat16)
    upsampled = jnp.einsum(
        "joc,kcrw->kjrow", upsample_weight, activated, preferred_element_type=jnp.float32
    )
    upsampled = upsampled.reshape(-1, rows + 2, channels, columns).astype(jnp.bfloat16)
    band = lax.axis_index("rows")
    bands = lax.axis_size("rows")
    row_ids = lax.broadcasted_iota(jnp.int32, (1, rows + 2, 1, 1), 1)
    inside = ((row_ids > 0) | (band > 0)) & ((row_ids < rows + 1) | (band < bands - 1))
    upsampled = jnp.where(inside, upsampled, jnp.zeros_like(upsampled))
    previous = upsampled[frames - 2 : frames]
    previous = jnp.where(lax.axis_index("tm") > 0, previous, jnp.zeros_like(previous))
    rebuilt_flat = pl.pallas_call(
        functools.partial(rebuild_kernel, **dims),
        out_shape=jax.ShapeDtypeStruct((frames, channels, rows * columns), jnp.bfloat16),
    )(jnp.concatenate([previous, upsampled[frames:]], 0), merged_kernel(final_kernel))
    rebuilt = rebuilt_flat.reshape(frames, channels, rows, columns)
    return (latent, rebuilt)


def solution(mesh):
    return jax.shard_map(
        body,
        mesh=mesh,
        in_specs=(P("tm", None, "rows", None), P(), P(), P(), P(), P(), P(), P(), P(), P(), P()),
        out_specs=(P("tm", None, "rows", None), P("tm", None, "rows", None)),
        check_vma=False,
    )
```

```python
import functools

import jax
import jax.numpy as jnp
from jax import lax
from jax.experimental import pallas as pl
from jax.experimental.pallas import tpu as pltpu
from jax.sharding import PartitionSpec as P


def shift(x, dt, dr):
    nt = lax.axis_size("tm")
    nr = lax.axis_size("rows")
    if dt == 0:
        pairs = [(r, r + dr) for r in range(nr) if 0 <= r + dr < nr]
        return lax.ppermute(x, "rows", pairs)
    if dr == 0:
        pairs = [(t, t + dt) for t in range(nt) if 0 <= t + dt < nt]
        return lax.ppermute(x, "tm", pairs)
    pairs = [
        (t * nr + r, (t + dt) * nr + r + dr)
        for t in range(nt)
        for r in range(nr)
        if 0 <= t + dt < nt and 0 <= r + dr < nr
    ]
    return lax.ppermute(x, ("tm", "rows"), pairs)


def haloed_rows_first(v):
    prev = shift(v[-2:], 1, 0)
    top = shift(v[:, -1:], 0, 1)
    bottom = shift(v[:, :1], 0, -1)
    top_corner = shift(v[-2:, -1:], 1, 1)
    bottom_corner = shift(v[-2:, :1], 1, -1)
    own = jnp.concatenate([top, v, bottom], 1)
    before = jnp.concatenate([top_corner, prev, bottom_corner], 1)
    return jnp.concatenate([before, own], 0)


def merged_kernel(kernel):
    o, c = kernel.shape[3], kernel.shape[4]
    return kernel.transpose(2, 3, 0, 1, 4).reshape(3 * o, 9 * c)


def tap_sum(x_ref, k_ref, t, rows, columns):
    pieces = []
    for a in range(3):
        for b in range(3):
            pieces.append(
                jnp.concatenate([x_ref[t + a, r + b] for r in range(rows)], axis=1)
            )
    stacked = jnp.concatenate(pieces, axis=0)
    acc = jnp.dot(k_ref[...], stacked, preferred_element_type=jnp.float32)
    out_channels = acc.shape[0] // 3
    width = rows * columns
    lane = lax.broadcasted_iota(jnp.int32, (out_channels, width), 1) % columns
    left = pltpu.roll(acc[:out_channels], 1, 1)
    right = pltpu.roll(acc[2 * out_channels :], width - 1, 1)
    left = jnp.where(lane == 0, 0.0, left)
    right = jnp.where(lane == columns - 1, 0.0, right)
    return left + acc[out_channels : 2 * out_channels] + right


def gate_kernel(x_ref, k_ref, bias_ref, gain_ref, o_ref, *, frames, rows, columns):
    bias = bias_ref[...]
    gain = gain_ref[...]
    for t in range(frames):
        y = tap_sum(x_ref, k_ref, t, rows, columns) + bias
        scale = lax.rsqrt(jnp.mean(y * y, axis=0, keepdims=True) + 1e-06)
        z = y * scale * gain
        g = (z / (1.0 + jnp.exp(-z))).astype(o_ref.dtype)
        for r in range(rows):
            o_ref[t, r] = g[:, r * columns : (r + 1) * columns]


def latent_kernel(x_ref, k_ref, res_ref, w_ref, o_ref, *, frames, rows, columns):
    total = None
    for t in range(frames):
        y = tap_sum(x_ref, k_ref, t, rows, columns)
        res = jnp.concatenate([res_ref[t, r] for r in range(rows)], axis=1)
        hidden = (res.astype(jnp.float32) + y).astype(jnp.bfloat16)
        part = jnp.dot(w_ref[t], hidden, preferred_element_type=jnp.float32)
        total = part if total is None else total + part
    for r in range(rows):
        o_ref[r] = total[:, r * columns : (r + 1) * columns].astype(o_ref.dtype)


def decode_kernel_body(
    lat_ref, dk_ref, bias_ref, gain_ref, up_ref, mask_ref, fk_ref, o_ref, ext_ref,
    *, frames, rows, columns
):
    wide = rows + 2
    bias = bias_ref[...]
    gain = gain_ref[...]
    for f in range(2):
        y = tap_sum(lat_ref, dk_ref, f, wide, columns) + bias
        scale = lax.rsqrt(jnp.mean(y * y, axis=0, keepdims=True) + 1e-06)
        z = y * scale * gain
        act = (z / (1.0 + jnp.exp(-z))).astype(jnp.bfloat16)
        first_j = frames - 2 if f == 0 else 0
        for j in range(first_j, frames):
            up = jnp.dot(up_ref[j], act, preferred_element_type=jnp.float32)
            slot = j - first_j if f == 0 else j + 2
            for r in range(wide):
                piece = up[:, r * columns : (r + 1) * columns] * mask_ref[slot, r]
                ext_ref[slot, r] = piece.astype(ext_ref.dtype)
    for t in range(frames):
        y = tap_sum(ext_ref, fk_ref, t, rows, columns)
        res = jnp.concatenate([ext_ref[t + 2, r + 1] for r in range(rows)], axis=1)
        o_ref[t] = (res.astype(jnp.float32) + y).astype(o_ref.dtype)


def normed_silu(values, gain):
    scale = lax.rsqrt(jnp.mean(values * values, axis=1, keepdims=True) + 1e-06)
    return jax.nn.silu(values * scale * gain[None, :, None, None])


def conv_valid(v, kernel):
    out = lax.conv_general_dilated(
        v[None],
        kernel,
        (1, 1, 1),
        [(0, 0), (0, 0), (1, 1)],
        dimension_numbers=("NDCHW", "DHWOI", "NDCHW"),
        preferred_element_type=jnp.float32,
    )
    return out[0]


def body(
    features,
    first_kernel,
    first_bias,
    first_gain,
    second_kernel,
    latent_weight,
    decode_kernel,
    decode_bias,
    decode_gain,
    upsample_weight,
    final_kernel,
):
    frames, channels, rows, columns = features.shape
    z_count = latent_weight.shape[1]
    dims = dict(frames=frames, rows=rows, columns=columns)
    own = features.transpose(0, 2, 1, 3)
    gated = pl.pallas_call(
        functools.partial(gate_kernel, **dims),
        out_shape=jax.ShapeDtypeStruct((frames, rows, channels, columns), jnp.bfloat16),
    )(
        haloed_rows_first(own),
        merged_kernel(first_kernel),
        first_bias[:, None],
        first_gain[:, None],
    )
    lat = pl.pallas_call(
        functools.partial(latent_kernel, **dims),
        out_shape=jax.ShapeDtypeStruct((rows, z_count, columns), jnp.bfloat16),
    )(haloed_rows_first(gated), merged_kernel(second_kernel), own, latent_weight)
    latent = lat.transpose(1, 0, 2)[None]
    stacked = jnp.stack(
        [
            jnp.concatenate(
                [shift(lat[-2:], dt, 1), lat if dt == 0 else shift(lat, dt, 0), shift(lat[:2], dt, -1)],
                0,
            )
            for dt in (3, 2, 1, 0)
        ],
        0,
    )
    band = lax.axis_index("rows")
    bands = lax.axis_size("rows")
    row_ids = lax.broadcasted_iota(jnp.int32, (frames + 2, rows + 2), 1)
    frame_ids = lax.broadcasted_iota(jnp.int32, (frames + 2, rows + 2), 0)
    inside = ((row_ids > 0) | (band > 0)) & ((row_ids < rows + 1) | (band < bands - 1))
    inside = inside & ((frame_ids >= 2) | (lax.axis_index("tm") > 0))
    mask = inside.astype(jnp.float32)
    vmem = pl.BlockSpec(memory_space=pltpu.VMEM)
    rebuilt_flat = pl.pallas_call(
        functools.partial(decode_kernel_body, **dims),
        out_shape=jax.ShapeDtypeStruct((frames, channels, rows * columns), jnp.bfloat16),
        in_specs=[vmem] * 5 + [pl.BlockSpec(memory_space=pltpu.SMEM), vmem],
        scratch_shapes=[pltpu.VMEM((frames + 2, rows + 2, channels, columns), jnp.bfloat16)],
    )(
        stacked,
        merged_kernel(decode_kernel),
        decode_bias[:, None],
        decode_gain[:, None],
        upsample_weight,
        mask,
        merged_kernel(final_kernel),
    )
    rebuilt = rebuilt_flat.reshape(frames, channels, rows, columns)
    return (latent, rebuilt)


def solution(mesh):
    return jax.shard_map(
        body,
        mesh=mesh,
        in_specs=(P("tm", None, "rows", None), P(), P(), P(), P(), P(), P(), P(), P(), P(), P()),
        out_specs=(P("tm", None, "rows", None), P("tm", None, "rows", None)),
        check_vma=False,
    )
```

```python
import functools

import jax
import jax.numpy as jnp
from jax import lax
from jax.experimental import pallas as pl
from jax.experimental.pallas import tpu as pltpu
from jax.sharding import PartitionSpec as P


def shift(x, dt, dr):
    nt = lax.axis_size("tm")
    nr = lax.axis_size("rows")
    if dt == 0:
        pairs = [(r, r + dr) for r in range(nr) if 0 <= r + dr < nr]
        return lax.ppermute(x, "rows", pairs)
    if dr == 0:
        pairs = [(t, t + dt) for t in range(nt) if 0 <= t + dt < nt]
        return lax.ppermute(x, "tm", pairs)
    pairs = [
        (t * nr + r, (t + dt) * nr + r + dr)
        for t in range(nt)
        for r in range(nr)
        if 0 <= t + dt < nt and 0 <= r + dr < nr
    ]
    return lax.ppermute(x, ("tm", "rows"), pairs)


def merged_kernel(kernel):
    o, c = kernel.shape[3], kernel.shape[4]
    return kernel.transpose(2, 3, 0, 1, 4).reshape(3 * o, 9 * c)


def tap_sum(x_ref, k_ref, t, rows, columns):
    pieces = []
    for a in range(3):
        for b in range(3):
            pieces.append(
                jnp.concatenate([x_ref[t + a, r + b] for r in range(rows)], axis=1)
            )
    stacked = jnp.concatenate(pieces, axis=0)
    acc = jnp.dot(k_ref[...], stacked, preferred_element_type=jnp.float32)
    out_channels = acc.shape[0] // 3
    width = rows * columns
    lane = lax.broadcasted_iota(jnp.int32, (out_channels, width), 1) % columns
    left = pltpu.roll(acc[:out_channels], 1, 1)
    right = pltpu.roll(acc[2 * out_channels :], width - 1, 1)
    left = jnp.where(lane == 0, 0.0, left)
    right = jnp.where(lane == columns - 1, 0.0, right)
    return left + acc[out_channels : 2 * out_channels] + right


def encoder_kernel(
    x_ref, k1_ref, bias_ref, gain_ref, mask_ref, k2_ref, w_ref, o_ref, g_ref,
    *, frames, rows, columns
):
    wide = rows + 2
    bias = bias_ref[...]
    gain = gain_ref[...]
    for t in range(frames + 2):
        y = tap_sum(x_ref, k1_ref, t, wide, columns) + bias
        scale = lax.rsqrt(jnp.mean(y * y, axis=0, keepdims=True) + 1e-06)
        z = y * scale * gain
        g = z / (1.0 + jnp.exp(-z))
        for r in range(wide):
            piece = g[:, r * columns : (r + 1) * columns] * mask_ref[t, r]
            g_ref[t, r] = piece.astype(g_ref.dtype)
    total = None
    for t in range(frames):
        y = tap_sum(g_ref, k2_ref, t, rows, columns)
        res = jnp.concatenate([x_ref[t + 4, r + 2] for r in range(rows)], axis=1)
        hidden = (res.astype(jnp.float32) + y).astype(jnp.bfloat16)
        part = jnp.dot(w_ref[t], hidden, preferred_element_type=jnp.float32)
        total = part if total is None else total + part
    for r in range(rows):
        o_ref[r] = total[:, r * columns : (r + 1) * columns].astype(o_ref.dtype)


def decode_kernel_body(
    lat_ref, dk_ref, bias_ref, gain_ref, up_ref, mask_ref, fk_ref, o_ref, ext_ref,
    *, frames, rows, columns
):
    wide = rows + 2
    bias = bias_ref[...]
    gain = gain_ref[...]
    for f in range(2):
        y = tap_sum(lat_ref, dk_ref, f, wide, columns) + bias
        scale = lax.rsqrt(jnp.mean(y * y, axis=0, keepdims=True) + 1e-06)
        z = y * scale * gain
        act = (z / (1.0 + jnp.exp(-z))).astype(jnp.bfloat16)
        first_j = frames - 2 if f == 0 else 0
        for j in range(first_j, frames):
            up = jnp.dot(up_ref[j], act, preferred_element_type=jnp.float32)
            slot = j - first_j if f == 0 else j + 2
            for r in range(wide):
                piece = up[:, r * columns : (r + 1) * columns] * mask_ref[slot, r]
                ext_ref[slot, r] = piece.astype(ext_ref.dtype)
    for t in range(frames):
        y = tap_sum(ext_ref, fk_ref, t, rows, columns)
        res = jnp.concatenate([ext_ref[t + 2, r + 1] for r in range(rows)], axis=1)
        o_ref[t] = (res.astype(jnp.float32) + y).astype(o_ref.dtype)


def body(
    features,
    first_kernel,
    first_bias,
    first_gain,
    second_kernel,
    latent_weight,
    decode_kernel,
    decode_bias,
    decode_gain,
    upsample_weight,
    final_kernel,
):
    frames, channels, rows, columns = features.shape
    z_count = latent_weight.shape[1]
    dims = dict(frames=frames, rows=rows, columns=columns)
    own = features.transpose(0, 2, 1, 3)
    ext = jnp.concatenate(
        [
            jnp.concatenate([shift(own[:, -2:], 1, 1), shift(own, 1, 0), shift(own[:, :2], 1, -1)], 1),
            jnp.concatenate([shift(own[:, -2:], 0, 1), own, shift(own[:, :2], 0, -1)], 1),
        ],
        0,
    )
    band = lax.axis_index("rows")
    bands = lax.axis_size("rows")
    row_ids = lax.broadcasted_iota(jnp.int32, (frames + 2, rows + 2), 1)
    frame_ids = lax.broadcasted_iota(jnp.int32, (frames + 2, rows + 2), 0)
    inside = ((row_ids > 0) | (band > 0)) & ((row_ids < rows + 1) | (band < bands - 1))
    inside = inside & ((frame_ids >= 2) | (lax.axis_index("tm") > 0))
    mask = inside.astype(jnp.float32)
    vmem = pl.BlockSpec(memory_space=pltpu.VMEM)
    smem = pl.BlockSpec(memory_space=pltpu.SMEM)
    lat = pl.pallas_call(
        functools.partial(encoder_kernel, **dims),
        out_shape=jax.ShapeDtypeStruct((rows, z_count, columns), jnp.bfloat16),
        in_specs=[vmem] * 4 + [smem, vmem, vmem],
        scratch_shapes=[pltpu.VMEM((frames + 2, rows + 2, channels, columns), jnp.bfloat16)],
    )(
        ext,
        merged_kernel(first_kernel),
        first_bias[:, None],
        first_gain[:, None],
        mask,
        merged_kernel(second_kernel),
        latent_weight,
    )
    latent = lat.transpose(1, 0, 2)[None]
    lat_rows = jnp.concatenate([shift(lat[-2:], 0, 1), lat, shift(lat[:2], 0, -1)], 0)
    stacked = jnp.stack(
        [shift(lat_rows, 3, 0), shift(lat_rows, 2, 0), shift(lat_rows, 1, 0), lat_rows], 0
    )
    rebuilt_flat = pl.pallas_call(
        functools.partial(decode_kernel_body, **dims),
        out_shape=jax.ShapeDtypeStruct((frames, channels, rows * columns), jnp.bfloat16),
        in_specs=[vmem] * 5 + [smem, vmem],
        scratch_shapes=[pltpu.VMEM((frames + 2, rows + 2, channels, columns), jnp.bfloat16)],
    )(
        stacked,
        merged_kernel(decode_kernel),
        decode_bias[:, None],
        decode_gain[:, None],
        upsample_weight,
        mask,
        merged_kernel(final_kernel),
    )
    rebuilt = rebuilt_flat.reshape(frames, channels, rows, columns)
    return (latent, rebuilt)


def solution(mesh):
    return jax.shard_map(
        body,
        mesh=mesh,
        in_specs=(P("tm", None, "rows", None), P(), P(), P(), P(), P(), P(), P(), P(), P(), P()),
        out_specs=(P("tm", None, "rows", None), P("tm", None, "rows", None)),
        check_vma=False,
    )
```

```python
import functools

import jax
import jax.numpy as jnp
from jax import lax
from jax.experimental import pallas as pl
from jax.experimental.pallas import tpu as pltpu
from jax.sharding import PartitionSpec as P


def shift(x, dt, dr):
    nt = lax.axis_size("tm")
    nr = lax.axis_size("rows")
    if dt == 0:
        pairs = [(r, r + dr) for r in range(nr) if 0 <= r + dr < nr]
        return lax.ppermute(x, "rows", pairs)
    if dr == 0:
        pairs = [(t, t + dt) for t in range(nt) if 0 <= t + dt < nt]
        return lax.ppermute(x, "tm", pairs)
    pairs = [
        (t * nr + r, (t + dt) * nr + r + dr)
        for t in range(nt)
        for r in range(nr)
        if 0 <= t + dt < nt and 0 <= r + dr < nr
    ]
    return lax.ppermute(x, ("tm", "rows"), pairs)


def merged_kernel(kernel):
    o, c = kernel.shape[3], kernel.shape[4]
    return kernel.transpose(2, 3, 0, 1, 4).reshape(3 * o, 9 * c)


def frame_rows(get, t, r0, rows):
    return jnp.concatenate([get(t, r0 + r) for r in range(rows)], axis=1)


def from_ref(x_ref):
    return lambda t, r: x_ref[t, r]


def tiled(parts, frames_each, rows_top, rows_mid):
    def get(t, r):
        block = parts[t // frames_each]
        f = t % frames_each
        if r < rows_top:
            return block[0][f, :, r, :]
        if r < rows_top + rows_mid:
            return block[1][f, :, r - rows_top, :]
        return block[2][f, :, r - rows_top - rows_mid, :]

    return get


def tap_sum(get, k_ref, t, rows, columns):
    pieces = []
    for a in range(3):
        for b in range(3):
            pieces.append(frame_rows(get, t + a, b, rows))
    stacked = jnp.concatenate(pieces, axis=0)
    acc = jnp.dot(k_ref[...], stacked, preferred_element_type=jnp.float32)
    out_channels = acc.shape[0] // 3
    width = rows * columns
    lane = lax.broadcasted_iota(jnp.int32, (out_channels, width), 1) % columns
    left = pltpu.roll(acc[:out_channels], 1, 1)
    right = pltpu.roll(acc[2 * out_channels :], width - 1, 1)
    left = jnp.where(lane == 0, 0.0, left)
    right = jnp.where(lane == columns - 1, 0.0, right)
    return left + acc[out_channels : 2 * out_channels] + right


def encoder_kernel(
    tc_ref, pv_ref, bc_ref, tp_ref, own_ref, bt_ref,
    k1_ref, bias_ref, gain_ref, mask_ref, k2_ref, w_ref, o_ref, g_ref,
    *, frames, rows, columns
):
    wide = rows + 2
    bias = bias_ref[...]
    gain = gain_ref[...]
    x = tiled([(tc_ref, pv_ref, bc_ref), (tp_ref, own_ref, bt_ref)], frames, 2, rows)
    for t in range(frames + 2):
        y = tap_sum(x, k1_ref, t, wide, columns) + bias
        scale = lax.rsqrt(jnp.mean(y * y, axis=0, keepdims=True) + 1e-06)
        z = y * scale * gain
        g = z / (1.0 + jnp.exp(-z))
        for r in range(wide):
            piece = g[:, r * columns : (r + 1) * columns] * mask_ref[t, r]
            g_ref[t, r] = piece.astype(g_ref.dtype)
    total = None
    for t in range(frames):
        y = tap_sum(from_ref(g_ref), k2_ref, t, rows, columns)
        res = frame_rows(x, t + frames, 2, rows)
        hidden = (res.astype(jnp.float32) + y).astype(jnp.bfloat16)
        part = jnp.dot(w_ref[t], hidden, preferred_element_type=jnp.float32)
        total = part if total is None else total + part
    for r in range(rows):
        o_ref[0, :, r, :] = total[:, r * columns : (r + 1) * columns].astype(o_ref.dtype)


def decode_kernel_body(
    l3_ref, l2_ref, l1_ref, l0_ref, dk_ref, bias_ref, gain_ref, up_ref, mask_ref, fk_ref, o_ref, ext_ref,
    *, frames, rows, columns
):
    wide = rows + 2
    bias = bias_ref[...]
    gain = gain_ref[...]
    lat_refs = (l3_ref, l2_ref, l1_ref, l0_ref)
    lat = lambda t, r: lat_refs[t][0, :, r, :]
    for f in range(2):
        y = tap_sum(lat, dk_ref, f, wide, columns) + bias
        scale = lax.rsqrt(jnp.mean(y * y, axis=0, keepdims=True) + 1e-06)
        z = y * scale * gain
        act = (z / (1.0 + jnp.exp(-z))).astype(jnp.bfloat16)
        first_j = frames - 2 if f == 0 else 0
        for j in range(first_j, frames):
            up = jnp.dot(up_ref[j], act, preferred_element_type=jnp.float32)
            slot = j - first_j if f == 0 else j + 2
            for r in range(wide):
                piece = up[:, r * columns : (r + 1) * columns] * mask_ref[slot, r]
                ext_ref[slot, r] = piece.astype(ext_ref.dtype)
    for t in range(frames):
        y = tap_sum(from_ref(ext_ref), fk_ref, t, rows, columns)
        res = frame_rows(from_ref(ext_ref), t + 2, 1, rows)
        out = (res.astype(jnp.float32) + y).astype(o_ref.dtype)
        for r in range(rows):
            o_ref[t, :, r, :] = out[:, r * columns : (r + 1) * columns]


def body(
    features,
    first_kernel,
    first_bias,
    first_gain,
    second_kernel,
    latent_weight,
    decode_kernel,
    decode_bias,
    decode_gain,
    upsample_weight,
    final_kernel,
):
    frames, channels, rows, columns = features.shape
    z_count = latent_weight.shape[1]
    dims = dict(frames=frames, rows=rows, columns=columns)
    top = features[:, :, -2:]
    bottom = features[:, :, :2]
    pieces = [
        shift(top, 1, 1),
        shift(features, 1, 0),
        shift(bottom, 1, -1),
        shift(top, 0, 1),
        features,
        shift(bottom, 0, -1),
    ]
    band = lax.axis_index("rows")
    bands = lax.axis_size("rows")
    row_ids = lax.broadcasted_iota(jnp.int32, (frames + 2, rows + 2), 1)
    frame_ids = lax.broadcasted_iota(jnp.int32, (frames + 2, rows + 2), 0)
    inside = ((row_ids > 0) | (band > 0)) & ((row_ids < rows + 1) | (band < bands - 1))
    inside = inside & ((frame_ids >= 2) | (lax.axis_index("tm") > 0))
    mask = inside.astype(jnp.float32)
    vmem = pl.BlockSpec(memory_space=pltpu.VMEM)
    smem = pl.BlockSpec(memory_space=pltpu.SMEM)
    latent = pl.pallas_call(
        functools.partial(encoder_kernel, **dims),
        out_shape=jax.ShapeDtypeStruct((1, z_count, rows, columns), jnp.bfloat16),
        in_specs=[vmem] * 9 + [smem, vmem, vmem],
        scratch_shapes=[pltpu.VMEM((frames + 2, rows + 2, channels, columns), jnp.bfloat16)],
    )(
        *pieces,
        merged_kernel(first_kernel),
        first_bias[:, None],
        first_gain[:, None],
        mask,
        merged_kernel(second_kernel),
        latent_weight,
    )
    lat_rows = jnp.concatenate(
        [shift(latent[:, :, -2:], 0, 1), latent, shift(latent[:, :, :2], 0, -1)], 2
    )
    lat_frames = [shift(lat_rows, 3, 0), shift(lat_rows, 2, 0), shift(lat_rows, 1, 0), lat_rows]
    rebuilt = pl.pallas_call(
        functools.partial(decode_kernel_body, **dims),
        out_shape=jax.ShapeDtypeStruct((frames, channels, rows, columns), jnp.bfloat16),
        in_specs=[vmem] * 8 + [smem, vmem],
        scratch_shapes=[pltpu.VMEM((frames + 2, rows + 2, channels, columns), jnp.bfloat16)],
    )(
        *lat_frames,
        merged_kernel(decode_kernel),
        decode_bias[:, None],
        decode_gain[:, None],
        upsample_weight,
        mask,
        merged_kernel(final_kernel),
    )
    return (latent, rebuilt)


def solution(mesh):
    return jax.shard_map(
        body,
        mesh=mesh,
        in_specs=(P("tm", None, "rows", None), P(), P(), P(), P(), P(), P(), P(), P(), P(), P()),
        out_specs=(P("tm", None, "rows", None), P("tm", None, "rows", None)),
        check_vma=False,
    )
```

```python
import functools

import jax
import jax.numpy as jnp
from jax import lax
from jax.experimental import pallas as pl
from jax.experimental.pallas import tpu as pltpu
from jax.sharding import PartitionSpec as P


def shift(x, dt, dr):
    nt = lax.axis_size("tm")
    nr = lax.axis_size("rows")
    if dt == 0:
        pairs = [(r, r + dr) for r in range(nr) if 0 <= r + dr < nr]
        return lax.ppermute(x, "rows", pairs)
    if dr == 0:
        pairs = [(t, t + dt) for t in range(nt) if 0 <= t + dt < nt]
        return lax.ppermute(x, "tm", pairs)
    pairs = [
        (t * nr + r, (t + dt) * nr + r + dr)
        for t in range(nt)
        for r in range(nr)
        if 0 <= t + dt < nt and 0 <= r + dr < nr
    ]
    return lax.ppermute(x, ("tm", "rows"), pairs)


def merged_kernel(kernel):
    o, c = kernel.shape[3], kernel.shape[4]
    return kernel.transpose(2, 3, 0, 1, 4).reshape(3 * o, 9 * c)


def frame_rows(get, t, r0, rows):
    return jnp.concatenate([get(t, r0 + r) for r in range(rows)], axis=1)


def from_ref(x_ref):
    return lambda t, r: x_ref[t, r]


def tiled(parts, frames_each, rows_top, rows_mid):
    def get(t, r):
        block = parts[t // frames_each]
        f = t % frames_each
        if r < rows_top:
            return block[0][f, r]
        if r < rows_top + rows_mid:
            return block[1][f, r - rows_top]
        return block[2][f, r - rows_top - rows_mid]

    return get


def tap_sum(get, k_ref, t, rows, columns):
    pieces = []
    for a in range(3):
        for b in range(3):
            pieces.append(frame_rows(get, t + a, b, rows))
    stacked = jnp.concatenate(pieces, axis=0)
    acc = jnp.dot(k_ref[...], stacked, preferred_element_type=jnp.float32)
    out_channels = acc.shape[0] // 3
    width = rows * columns
    lane = lax.broadcasted_iota(jnp.int32, (out_channels, width), 1) % columns
    left = pltpu.roll(acc[:out_channels], 1, 1)
    right = pltpu.roll(acc[2 * out_channels :], width - 1, 1)
    left = jnp.where(lane == 0, 0.0, left)
    right = jnp.where(lane == columns - 1, 0.0, right)
    return left + acc[out_channels : 2 * out_channels] + right


def encoder_kernel(
    tc_ref, pv_ref, bc_ref, tp_ref, own_ref, bt_ref,
    k1_ref, bias_ref, gain_ref, mask_ref, k2_ref, w_ref, o_ref, g_ref,
    *, frames, rows, columns
):
    wide = rows + 2
    bias = bias_ref[...]
    gain = gain_ref[...]
    x = tiled([(tc_ref, pv_ref, bc_ref), (tp_ref, own_ref, bt_ref)], frames, 2, rows)
    for t in range(frames + 2):
        y = tap_sum(x, k1_ref, t, wide, columns) + bias
        scale = lax.rsqrt(jnp.mean(y * y, axis=0, keepdims=True) + 1e-06)
        z = y * scale * gain
        g = z / (1.0 + jnp.exp(-z))
        for r in range(wide):
            piece = g[:, r * columns : (r + 1) * columns] * mask_ref[t, r]
            g_ref[t, r] = piece.astype(g_ref.dtype)
    total = None
    for t in range(frames):
        y = tap_sum(from_ref(g_ref), k2_ref, t, rows, columns)
        res = frame_rows(x, t + frames, 2, rows)
        hidden = (res.astype(jnp.float32) + y).astype(jnp.bfloat16)
        part = jnp.dot(w_ref[t], hidden, preferred_element_type=jnp.float32)
        total = part if total is None else total + part
    for r in range(rows):
        o_ref[0, :, r, :] = total[:, r * columns : (r + 1) * columns].astype(o_ref.dtype)


def decode_kernel_body(
    l3_ref, l2_ref, l1_ref, l0_ref, dk_ref, bias_ref, gain_ref, up_ref, mask_ref, fk_ref, o_ref, ext_ref,
    *, frames, rows, columns
):
    wide = rows + 2
    bias = bias_ref[...]
    gain = gain_ref[...]
    lat_refs = (l3_ref, l2_ref, l1_ref, l0_ref)
    lat = lambda t, r: lat_refs[t][0, :, r, :]
    for f in range(2):
        y = tap_sum(lat, dk_ref, f, wide, columns) + bias
        scale = lax.rsqrt(jnp.mean(y * y, axis=0, keepdims=True) + 1e-06)
        z = y * scale * gain
        act = (z / (1.0 + jnp.exp(-z))).astype(jnp.bfloat16)
        first_j = frames - 2 if f == 0 else 0
        for j in range(first_j, frames):
            up = jnp.dot(up_ref[j], act, preferred_element_type=jnp.float32)
            slot = j - first_j if f == 0 else j + 2
            for r in range(wide):
                piece = up[:, r * columns : (r + 1) * columns] * mask_ref[slot, r]
                ext_ref[slot, r] = piece.astype(ext_ref.dtype)
    for t in range(frames):
        y = tap_sum(from_ref(ext_ref), fk_ref, t, rows, columns)
        res = frame_rows(from_ref(ext_ref), t + 2, 1, rows)
        out = (res.astype(jnp.float32) + y).astype(o_ref.dtype)
        for r in range(rows):
            o_ref[t, :, r, :] = out[:, r * columns : (r + 1) * columns]


def body(
    features,
    first_kernel,
    first_bias,
    first_gain,
    second_kernel,
    latent_weight,
    decode_kernel,
    decode_bias,
    decode_gain,
    upsample_weight,
    final_kernel,
):
    frames, channels, rows, columns = features.shape
    z_count = latent_weight.shape[1]
    dims = dict(frames=frames, rows=rows, columns=columns)
    own = features.transpose(0, 2, 1, 3)
    top = own[:, -2:]
    bottom = own[:, :2]
    pieces = [
        shift(top, 1, 1),
        shift(own, 1, 0),
        shift(bottom, 1, -1),
        shift(top, 0, 1),
        own,
        shift(bottom, 0, -1),
    ]
    band = lax.axis_index("rows")
    bands = lax.axis_size("rows")
    row_ids = lax.broadcasted_iota(jnp.int32, (frames + 2, rows + 2), 1)
    frame_ids = lax.broadcasted_iota(jnp.int32, (frames + 2, rows + 2), 0)
    inside = ((row_ids > 0) | (band > 0)) & ((row_ids < rows + 1) | (band < bands - 1))
    inside = inside & ((frame_ids >= 2) | (lax.axis_index("tm") > 0))
    mask = inside.astype(jnp.float32)
    vmem = pl.BlockSpec(memory_space=pltpu.VMEM)
    smem = pl.BlockSpec(memory_space=pltpu.SMEM)
    latent = pl.pallas_call(
        functools.partial(encoder_kernel, **dims),
        out_shape=jax.ShapeDtypeStruct((1, z_count, rows, columns), jnp.bfloat16),
        in_specs=[vmem] * 9 + [smem, vmem, vmem],
        scratch_shapes=[pltpu.VMEM((frames + 2, rows + 2, channels, columns), jnp.bfloat16)],
    )(
        *pieces,
        merged_kernel(first_kernel),
        first_bias[:, None],
        first_gain[:, None],
        mask,
        merged_kernel(second_kernel),
        latent_weight,
    )
    lat_rows = jnp.concatenate(
        [shift(latent[:, :, -2:], 0, 1), latent, shift(latent[:, :, :2], 0, -1)], 2
    )
    lat_frames = [shift(lat_rows, 3, 0), shift(lat_rows, 2, 0), shift(lat_rows, 1, 0), lat_rows]
    rebuilt = pl.pallas_call(
        functools.partial(decode_kernel_body, **dims),
        out_shape=jax.ShapeDtypeStruct((frames, channels, rows, columns), jnp.bfloat16),
        in_specs=[vmem] * 8 + [smem, vmem],
        scratch_shapes=[pltpu.VMEM((frames + 2, rows + 2, channels, columns), jnp.bfloat16)],
    )(
        *lat_frames,
        merged_kernel(decode_kernel),
        decode_bias[:, None],
        decode_gain[:, None],
        upsample_weight,
        mask,
        merged_kernel(final_kernel),
    )
    return (latent, rebuilt)


def solution(mesh):
    return jax.shard_map(
        body,
        mesh=mesh,
        in_specs=(P("tm", None, "rows", None), P(), P(), P(), P(), P(), P(), P(), P(), P(), P()),
        out_specs=(P("tm", None, "rows", None), P("tm", None, "rows", None)),
        check_vma=False,
    )
```

```python
import functools

import jax
import jax.numpy as jnp
from jax import lax
from jax.experimental import pallas as pl
from jax.experimental.pallas import tpu as pltpu
from jax.sharding import PartitionSpec as P


def shift(x, dt, dr):
    nt = lax.axis_size("tm")
    nr = lax.axis_size("rows")
    if dt == 0:
        pairs = [(r, r + dr) for r in range(nr) if 0 <= r + dr < nr]
        return lax.ppermute(x, "rows", pairs)
    if dr == 0:
        pairs = [(t, t + dt) for t in range(nt) if 0 <= t + dt < nt]
        return lax.ppermute(x, "tm", pairs)
    pairs = [
        (t * nr + r, (t + dt) * nr + r + dr)
        for t in range(nt)
        for r in range(nr)
        if 0 <= t + dt < nt and 0 <= r + dr < nr
    ]
    return lax.ppermute(x, ("tm", "rows"), pairs)


def merged_kernel(kernel):
    o, c = kernel.shape[3], kernel.shape[4]
    return kernel.transpose(2, 3, 0, 1, 4).reshape(3 * o, 9 * c)


def frame_rows(get, t, r0, rows):
    return jnp.concatenate([get(t, r0 + r) for r in range(rows)], axis=1)


def from_ref(x_ref):
    return lambda t, r: x_ref[t, r]


def tiled(parts, frames_each, rows_top, rows_mid):
    def get(t, r):
        block = parts[t // frames_each]
        f = t % frames_each
        if r < rows_top:
            return block[0][f, r]
        if r < rows_top + rows_mid:
            return block[1][f, r - rows_top]
        return block[2][f, r - rows_top - rows_mid]

    return get


def tap_sum(get, k_ref, t, rows, columns):
    pieces = []
    for a in range(3):
        for b in range(3):
            pieces.append(frame_rows(get, t + a, b, rows))
    stacked = jnp.concatenate(pieces, axis=0)
    acc = jnp.dot(k_ref[...], stacked, preferred_element_type=jnp.float32)
    out_channels = acc.shape[0] // 3
    width = rows * columns
    lane = lax.broadcasted_iota(jnp.int32, (out_channels, width), 1) % columns
    left = pltpu.roll(acc[:out_channels], 1, 1)
    right = pltpu.roll(acc[2 * out_channels :], width - 1, 1)
    left = jnp.where(lane == 0, 0.0, left)
    right = jnp.where(lane == columns - 1, 0.0, right)
    return left + acc[out_channels : 2 * out_channels] + right


def encoder_kernel(
    tc_ref, pv_ref, bc_ref, tp_ref, own_ref, bt_ref,
    k1_ref, bias_ref, gain_ref, mask_ref, k2_ref, w_ref, o_ref, g_ref,
    *, frames, rows, columns
):
    wide = rows + 2
    bias = bias_ref[...]
    gain = gain_ref[...]
    x = tiled([(tc_ref, pv_ref, bc_ref), (tp_ref, own_ref, bt_ref)], frames, 2, rows)
    for t in range(frames + 2):
        y = tap_sum(x, k1_ref, t, wide, columns) + bias
        scale = lax.rsqrt(jnp.mean(y * y, axis=0, keepdims=True) + 1e-06)
        z = y * scale * gain
        g = z / (1.0 + jnp.exp(-z))
        for r in range(wide):
            piece = g[:, r * columns : (r + 1) * columns] * mask_ref[t, r]
            g_ref[t, r] = piece.astype(g_ref.dtype)
    total = None
    for t in range(frames):
        y = tap_sum(from_ref(g_ref), k2_ref, t, rows, columns)
        res = frame_rows(x, t + frames, 2, rows)
        hidden = (res.astype(jnp.float32) + y).astype(jnp.bfloat16)
        part = jnp.dot(w_ref[t], hidden, preferred_element_type=jnp.float32)
        total = part if total is None else total + part
    for r in range(rows):
        o_ref[0, :, r, :] = total[:, r * columns : (r + 1) * columns].astype(o_ref.dtype)


def decode_kernel_body(
    l3_ref, l2_ref, l1_ref, l0_ref, dk_ref, bias_ref, gain_ref, up_ref, mask_ref, fk_ref, o_ref, ext_ref,
    *, frames, rows, columns
):
    wide = rows + 2
    bias = bias_ref[...]
    gain = gain_ref[...]
    lat_refs = (l3_ref, l2_ref, l1_ref, l0_ref)
    lat = lambda t, r: lat_refs[t][0, :, r, :]
    for f in range(2):
        y = tap_sum(lat, dk_ref, f, wide, columns) + bias
        scale = lax.rsqrt(jnp.mean(y * y, axis=0, keepdims=True) + 1e-06)
        z = y * scale * gain
        act = (z / (1.0 + jnp.exp(-z))).astype(jnp.bfloat16)
        first_j = frames - 2 if f == 0 else 0
        for j in range(first_j, frames):
            up = jnp.dot(up_ref[j], act, preferred_element_type=jnp.float32)
            slot = j - first_j if f == 0 else j + 2
            for r in range(wide):
                piece = up[:, r * columns : (r + 1) * columns] * mask_ref[slot, r]
                ext_ref[slot, r] = piece.astype(ext_ref.dtype)
    for t in range(frames):
        y = tap_sum(from_ref(ext_ref), fk_ref, t, rows, columns)
        res = frame_rows(from_ref(ext_ref), t + 2, 1, rows)
        out = (res.astype(jnp.float32) + y).astype(o_ref.dtype)
        for r in range(rows):
            o_ref[t, :, r, :] = out[:, r * columns : (r + 1) * columns]


def body(
    features,
    first_kernel,
    first_bias,
    first_gain,
    second_kernel,
    latent_weight,
    decode_kernel,
    decode_bias,
    decode_gain,
    upsample_weight,
    final_kernel,
):
    frames, channels, rows, columns = features.shape
    z_count = latent_weight.shape[1]
    dims = dict(frames=frames, rows=rows, columns=columns)
    own = features.transpose(0, 2, 1, 3)
    top = own[:, -2:]
    bottom = own[:, :2]
    previous = shift(own, 1, 0)
    pieces = [
        shift(previous[:, -2:], 0, 1),
        previous,
        shift(previous[:, :2], 0, -1),
        shift(top, 0, 1),
        own,
        shift(bottom, 0, -1),
    ]
    band = lax.axis_index("rows")
    bands = lax.axis_size("rows")
    row_ids = lax.broadcasted_iota(jnp.int32, (frames + 2, rows + 2), 1)
    frame_ids = lax.broadcasted_iota(jnp.int32, (frames + 2, rows + 2), 0)
    inside = ((row_ids > 0) | (band > 0)) & ((row_ids < rows + 1) | (band < bands - 1))
    inside = inside & ((frame_ids >= 2) | (lax.axis_index("tm") > 0))
    mask = inside.astype(jnp.float32)
    vmem = pl.BlockSpec(memory_space=pltpu.VMEM)
    smem = pl.BlockSpec(memory_space=pltpu.SMEM)
    latent = pl.pallas_call(
        functools.partial(encoder_kernel, **dims),
        out_shape=jax.ShapeDtypeStruct((1, z_count, rows, columns), jnp.bfloat16),
        in_specs=[vmem] * 9 + [smem, vmem, vmem],
        scratch_shapes=[pltpu.VMEM((frames + 2, rows + 2, channels, columns), jnp.bfloat16)],
    )(
        *pieces,
        merged_kernel(first_kernel),
        first_bias[:, None],
        first_gain[:, None],
        mask,
        merged_kernel(second_kernel),
        latent_weight,
    )
    lat_rows = jnp.concatenate(
        [shift(latent[:, :, -2:], 0, 1), latent, shift(latent[:, :, :2], 0, -1)], 2
    )
    lat_frames = [shift(lat_rows, 3, 0), shift(lat_rows, 2, 0), shift(lat_rows, 1, 0), lat_rows]
    rebuilt = pl.pallas_call(
        functools.partial(decode_kernel_body, **dims),
        out_shape=jax.ShapeDtypeStruct((frames, channels, rows, columns), jnp.bfloat16),
        in_specs=[vmem] * 8 + [smem, vmem],
        scratch_shapes=[pltpu.VMEM((frames + 2, rows + 2, channels, columns), jnp.bfloat16)],
    )(
        *lat_frames,
        merged_kernel(decode_kernel),
        decode_bias[:, None],
        decode_gain[:, None],
        upsample_weight,
        mask,
        merged_kernel(final_kernel),
    )
    return (latent, rebuilt)


def solution(mesh):
    return jax.shard_map(
        body,
        mesh=mesh,
        in_specs=(P("tm", None, "rows", None), P(), P(), P(), P(), P(), P(), P(), P(), P(), P()),
        out_specs=(P("tm", None, "rows", None), P("tm", None, "rows", None)),
        check_vma=False,
    )
```

```python
import functools

import jax
import jax.numpy as jnp
from jax import lax
from jax.experimental import pallas as pl
from jax.experimental.pallas import tpu as pltpu
from jax.sharding import PartitionSpec as P


def shift(x, dt, dr):
    nt = lax.axis_size("tm")
    nr = lax.axis_size("rows")
    if dt == 0:
        pairs = [(r, r + dr) for r in range(nr) if 0 <= r + dr < nr]
        return lax.ppermute(x, "rows", pairs)
    if dr == 0:
        pairs = [(t, t + dt) for t in range(nt) if 0 <= t + dt < nt]
        return lax.ppermute(x, "tm", pairs)
    pairs = [
        (t * nr + r, (t + dt) * nr + r + dr)
        for t in range(nt)
        for r in range(nr)
        if 0 <= t + dt < nt and 0 <= r + dr < nr
    ]
    return lax.ppermute(x, ("tm", "rows"), pairs)


def merged_kernel(kernel):
    o, c = kernel.shape[3], kernel.shape[4]
    return kernel.transpose(2, 3, 0, 1, 4).reshape(3 * o, 9 * c)


def frame_rows(get, t, r0, rows):
    return jnp.concatenate([get(t, r0 + r) for r in range(rows)], axis=1)


def from_ref(x_ref):
    return lambda t, r: x_ref[t, r]


def tiled(parts, frames_each, rows_top, rows_mid):
    def get(t, r):
        block = parts[t // frames_each]
        f = t % frames_each
        if r < rows_top:
            return block[0][f, r]
        if r < rows_top + rows_mid:
            return block[1][f, r - rows_top]
        return block[2][f, r - rows_top - rows_mid]

    return get


def tap_sum(get, k_ref, t, rows, columns):
    pieces = []
    for a in range(3):
        for b in range(3):
            pieces.append(frame_rows(get, t + a, b, rows))
    stacked = jnp.concatenate(pieces, axis=0)
    acc = jnp.dot(k_ref[...], stacked, preferred_element_type=jnp.float32)
    out_channels = acc.shape[0] // 3
    width = rows * columns
    lane = lax.broadcasted_iota(jnp.int32, (out_channels, width), 1) % columns
    left = pltpu.roll(acc[:out_channels], 1, 1)
    right = pltpu.roll(acc[2 * out_channels :], width - 1, 1)
    left = jnp.where(lane == 0, 0.0, left)
    right = jnp.where(lane == columns - 1, 0.0, right)
    return left + acc[out_channels : 2 * out_channels] + right


def encoder_kernel(
    tc_ref, pv_ref, bc_ref, tp_ref, own_ref, bt_ref,
    k1_ref, vec_ref, mask_ref, k2_ref, w_ref, o_ref, g_ref,
    *, frames, rows, columns
):
    wide = rows + 2
    bias = vec_ref[:, 0:1]
    gain = vec_ref[:, 1:2]
    x = tiled([(tc_ref, pv_ref, bc_ref), (tp_ref, own_ref, bt_ref)], frames, 2, rows)
    for t in range(frames + 2):
        y = tap_sum(x, k1_ref, t, wide, columns) + bias
        scale = lax.rsqrt(jnp.mean(y * y, axis=0, keepdims=True) + 1e-06)
        z = y * scale * gain
        g = z / (1.0 + jnp.exp(-z))
        for r in range(wide):
            piece = g[:, r * columns : (r + 1) * columns] * mask_ref[t, r]
            g_ref[t, r] = piece.astype(g_ref.dtype)
    total = None
    for t in range(frames):
        y = tap_sum(from_ref(g_ref), k2_ref, t, rows, columns)
        res = frame_rows(x, t + frames, 2, rows)
        hidden = (res.astype(jnp.float32) + y).astype(jnp.bfloat16)
        part = jnp.dot(w_ref[t], hidden, preferred_element_type=jnp.float32)
        total = part if total is None else total + part
    for r in range(rows):
        o_ref[0, :, r, :] = total[:, r * columns : (r + 1) * columns].astype(o_ref.dtype)


def decode_kernel_body(
    l3_ref, l2_ref, l1_ref, l0_ref, dk_ref, vec_ref, up_ref, mask_ref, fk_ref, o_ref, ext_ref,
    *, frames, rows, columns
):
    wide = rows + 2
    bias = vec_ref[:, 2:3]
    gain = vec_ref[:, 3:4]
    lat_refs = (l3_ref, l2_ref, l1_ref, l0_ref)
    lat = lambda t, r: lat_refs[t][0, :, r, :]
    for f in range(2):
        y = tap_sum(lat, dk_ref, f, wide, columns) + bias
        scale = lax.rsqrt(jnp.mean(y * y, axis=0, keepdims=True) + 1e-06)
        z = y * scale * gain
        act = (z / (1.0 + jnp.exp(-z))).astype(jnp.bfloat16)
        first_j = frames - 2 if f == 0 else 0
        for j in range(first_j, frames):
            up = jnp.dot(up_ref[j], act, preferred_element_type=jnp.float32)
            slot = j - first_j if f == 0 else j + 2
            for r in range(wide):
                piece = up[:, r * columns : (r + 1) * columns] * mask_ref[slot, r]
                ext_ref[slot, r] = piece.astype(ext_ref.dtype)
    for t in range(frames):
        y = tap_sum(from_ref(ext_ref), fk_ref, t, rows, columns)
        res = frame_rows(from_ref(ext_ref), t + 2, 1, rows)
        out = (res.astype(jnp.float32) + y).astype(o_ref.dtype)
        for r in range(rows):
            o_ref[t, :, r, :] = out[:, r * columns : (r + 1) * columns]


def body(
    features,
    first_kernel,
    first_bias,
    first_gain,
    second_kernel,
    latent_weight,
    decode_kernel,
    decode_bias,
    decode_gain,
    upsample_weight,
    final_kernel,
):
    frames, channels, rows, columns = features.shape
    z_count = latent_weight.shape[1]
    dims = dict(frames=frames, rows=rows, columns=columns)
    own = features.transpose(0, 2, 1, 3)
    top = own[:, -2:]
    bottom = own[:, :2]
    previous = shift(own, 1, 0)
    band = lax.axis_index("rows")
    bands = lax.axis_size("rows")
    row_ids = lax.broadcasted_iota(jnp.int32, (frames + 2, rows + 2), 1)
    frame_ids = lax.broadcasted_iota(jnp.int32, (frames + 2, rows + 2), 0)
    inside = ((row_ids > 0) | (band > 0)) & ((row_ids < rows + 1) | (band < bands - 1))
    inside = inside & ((frame_ids >= 2) | (lax.axis_index("tm") > 0))
    params = (
        merged_kernel(first_kernel),
        merged_kernel(second_kernel),
        merged_kernel(decode_kernel),
        merged_kernel(final_kernel),
        jnp.stack([first_bias, first_gain, decode_bias, decode_gain], 1),
        inside.astype(jnp.float32),
    )
    prev_top, prev_bottom, *params = lax.optimization_barrier(
        (previous[:, -2:], previous[:, :2], *params)
    )
    k1, k2, dk, fk, vec, mask = params
    pieces = [
        shift(prev_top, 0, 1),
        previous,
        shift(prev_bottom, 0, -1),
        shift(top, 0, 1),
        own,
        shift(bottom, 0, -1),
    ]
    vmem = pl.BlockSpec(memory_space=pltpu.VMEM)
    smem = pl.BlockSpec(memory_space=pltpu.SMEM)
    latent = pl.pallas_call(
        functools.partial(encoder_kernel, **dims),
        out_shape=jax.ShapeDtypeStruct((1, z_count, rows, columns), jnp.bfloat16),
        in_specs=[vmem] * 8 + [smem, vmem, vmem],
        scratch_shapes=[pltpu.VMEM((frames + 2, rows + 2, channels, columns), jnp.bfloat16)],
    )(
        *pieces,
        k1,
        vec,
        mask,
        k2,
        latent_weight,
    )
    lat_rows = jnp.concatenate(
        [shift(latent[:, :, -2:], 0, 1), latent, shift(latent[:, :, :2], 0, -1)], 2
    )
    lat_frames = [shift(lat_rows, 3, 0), shift(lat_rows, 2, 0), shift(lat_rows, 1, 0), lat_rows]
    rebuilt = pl.pallas_call(
        functools.partial(decode_kernel_body, **dims),
        out_shape=jax.ShapeDtypeStruct((frames, channels, rows, columns), jnp.bfloat16),
        in_specs=[vmem] * 7 + [smem, vmem],
        scratch_shapes=[pltpu.VMEM((frames + 2, rows + 2, channels, columns), jnp.bfloat16)],
    )(
        *lat_frames,
        dk,
        vec,
        upsample_weight,
        mask,
        fk,
    )
    return (latent, rebuilt)


def solution(mesh):
    return jax.shard_map(
        body,
        mesh=mesh,
        in_specs=(P("tm", None, "rows", None), P(), P(), P(), P(), P(), P(), P(), P(), P(), P()),
        out_specs=(P("tm", None, "rows", None), P("tm", None, "rows", None)),
        check_vma=False,
    )
```

```python
import functools

import jax
import jax.numpy as jnp
from jax import lax
from jax.experimental import pallas as pl
from jax.experimental.pallas import tpu as pltpu
from jax.sharding import PartitionSpec as P


def shift(x, dt, dr):
    nt = lax.axis_size("tm")
    nr = lax.axis_size("rows")
    if dt == 0:
        pairs = [(r, r + dr) for r in range(nr) if 0 <= r + dr < nr]
        return lax.ppermute(x, "rows", pairs)
    if dr == 0:
        pairs = [(t, t + dt) for t in range(nt) if 0 <= t + dt < nt]
        return lax.ppermute(x, "tm", pairs)
    pairs = [
        (t * nr + r, (t + dt) * nr + r + dr)
        for t in range(nt)
        for r in range(nr)
        if 0 <= t + dt < nt and 0 <= r + dr < nr
    ]
    return lax.ppermute(x, ("tm", "rows"), pairs)


def merged_kernel(kernel):
    o, c = kernel.shape[3], kernel.shape[4]
    return kernel.transpose(2, 3, 0, 1, 4).reshape(3 * o, 9 * c)


def frame_rows(get, t, r0, rows):
    return jnp.concatenate([get(t, r0 + r) for r in range(rows)], axis=1)


def from_ref(x_ref):
    return lambda t, r: x_ref[t, r]


def tiled(parts, frames_each, rows_top, rows_mid):
    def get(t, r):
        block = parts[t // frames_each]
        f = t % frames_each
        if r < rows_top:
            return block[0][f, r]
        if r < rows_top + rows_mid:
            return block[1][f, r - rows_top]
        return block[2][f, r - rows_top - rows_mid]

    return get


def tap_sum(get, k_ref, t, rows, columns):
    pieces = []
    for a in range(3):
        for b in range(3):
            pieces.append(frame_rows(get, t + a, b, rows))
    stacked = jnp.concatenate(pieces, axis=0)
    acc = jnp.dot(k_ref[...], stacked, preferred_element_type=jnp.float32)
    out_channels = acc.shape[0] // 3
    width = rows * columns
    lane = lax.broadcasted_iota(jnp.int32, (out_channels, width), 1) % columns
    left = pltpu.roll(acc[:out_channels], 1, 1)
    right = pltpu.roll(acc[2 * out_channels :], width - 1, 1)
    left = jnp.where(lane == 0, 0.0, left)
    right = jnp.where(lane == columns - 1, 0.0, right)
    return left + acc[out_channels : 2 * out_channels] + right


def encoder_kernel(
    tc_ref, pv_ref, bc_ref, tp_ref, own_ref, bt_ref,
    k1_ref, vec_ref, mask_ref, k2_ref, w_ref, o_ref, g_ref,
    *, frames, rows, columns
):
    wide = rows + 2
    bias = vec_ref[:, 0:1]
    gain = vec_ref[:, 1:2]
    x = tiled([(tc_ref, pv_ref, bc_ref), (tp_ref, own_ref, bt_ref)], frames, 2, rows)
    for t in range(frames + 2):
        y = tap_sum(x, k1_ref, t, wide, columns) + bias
        scale = lax.rsqrt(jnp.mean(y * y, axis=0, keepdims=True) + 1e-06)
        z = y * scale * gain
        g = z / (1.0 + jnp.exp(-z))
        for r in range(wide):
            piece = g[:, r * columns : (r + 1) * columns] * mask_ref[t, r]
            g_ref[t, r] = piece.astype(g_ref.dtype)
    total = None
    for t in range(frames):
        y = tap_sum(from_ref(g_ref), k2_ref, t, rows, columns)
        res = frame_rows(x, t + frames, 2, rows)
        hidden = (res.astype(jnp.float32) + y).astype(jnp.bfloat16)
        part = jnp.dot(w_ref[t], hidden, preferred_element_type=jnp.float32)
        total = part if total is None else total + part
    for r in range(rows):
        o_ref[0, :, r, :] = total[:, r * columns : (r + 1) * columns].astype(o_ref.dtype)


def decode_kernel_body(
    l3_ref, l2_ref, l1_ref, l0_ref, dk_ref, vec_ref, up_ref, mask_ref, fk_ref, o_ref, ext_ref,
    *, frames, rows, columns
):
    wide = rows + 2
    bias = vec_ref[:, 2:3]
    gain = vec_ref[:, 3:4]
    lat_refs = (l3_ref, l2_ref, l1_ref, l0_ref)
    lat = lambda t, r: lat_refs[t][0, :, r, :]
    for f in range(2):
        y = tap_sum(lat, dk_ref, f, wide, columns) + bias
        scale = lax.rsqrt(jnp.mean(y * y, axis=0, keepdims=True) + 1e-06)
        z = y * scale * gain
        act = (z / (1.0 + jnp.exp(-z))).astype(jnp.bfloat16)
        first_j = frames - 2 if f == 0 else 0
        for j in range(first_j, frames):
            up = jnp.dot(up_ref[j], act, preferred_element_type=jnp.float32)
            slot = j - first_j if f == 0 else j + 2
            for r in range(wide):
                piece = up[:, r * columns : (r + 1) * columns] * mask_ref[slot, r]
                ext_ref[slot, r] = piece.astype(ext_ref.dtype)
    for t in range(frames):
        y = tap_sum(from_ref(ext_ref), fk_ref, t, rows, columns)
        res = frame_rows(from_ref(ext_ref), t + 2, 1, rows)
        out = (res.astype(jnp.float32) + y).astype(o_ref.dtype)
        for r in range(rows):
            o_ref[t, :, r, :] = out[:, r * columns : (r + 1) * columns]


def body(
    features,
    first_kernel,
    first_bias,
    first_gain,
    second_kernel,
    latent_weight,
    decode_kernel,
    decode_bias,
    decode_gain,
    upsample_weight,
    final_kernel,
):
    frames, channels, rows, columns = features.shape
    z_count = latent_weight.shape[1]
    dims = dict(frames=frames, rows=rows, columns=columns)
    own = features.transpose(0, 2, 1, 3)
    top = own[:, -2:]
    bottom = own[:, :2]
    previous = shift(own, 1, 0)
    band = lax.axis_index("rows")
    bands = lax.axis_size("rows")
    row_ids = lax.broadcasted_iota(jnp.int32, (frames + 2, rows + 2), 1)
    frame_ids = lax.broadcasted_iota(jnp.int32, (frames + 2, rows + 2), 0)
    inside = ((row_ids > 0) | (band > 0)) & ((row_ids < rows + 1) | (band < bands - 1))
    inside = inside & ((frame_ids >= 2) | (lax.axis_index("tm") > 0))
    params = (
        merged_kernel(first_kernel),
        merged_kernel(second_kernel),
        merged_kernel(decode_kernel),
        merged_kernel(final_kernel),
        jnp.stack([first_bias, first_gain, decode_bias, decode_gain], 1),
        inside.astype(jnp.float32),
    )
    prev_top, prev_bottom, *params = lax.optimization_barrier(
        (previous[:, -2:], previous[:, :2], *params)
    )
    k1, k2, dk, fk, vec, mask = params
    pieces = [
        shift(prev_top, 0, 1),
        previous,
        shift(prev_bottom, 0, -1),
        shift(top, 0, 1),
        own,
        shift(bottom, 0, -1),
    ]
    vmem = pl.BlockSpec(memory_space=pltpu.VMEM)
    smem = pl.BlockSpec(memory_space=pltpu.SMEM)
    latent = pl.pallas_call(
        functools.partial(encoder_kernel, **dims),
        out_shape=jax.ShapeDtypeStruct((1, z_count, rows, columns), jnp.bfloat16),
        in_specs=[vmem] * 8 + [smem, vmem, vmem],
        scratch_shapes=[pltpu.VMEM((frames + 2, rows + 2, channels, columns), jnp.bfloat16)],
    )(
        *pieces,
        k1,
        vec,
        mask,
        k2,
        latent_weight,
    )
    lat_rows = jnp.concatenate(
        [shift(latent[:, :, -2:], 0, 1), latent, shift(latent[:, :, :2], 0, -1)], 2
    )
    lat_1 = shift(lat_rows, 1, 0)
    lat_32 = shift(jnp.concatenate([lat_1, lat_rows], 0), 2, 0)
    lat_frames = [lat_32[:1], lat_32[1:], lat_1, lat_rows]
    rebuilt = pl.pallas_call(
        functools.partial(decode_kernel_body, **dims),
        out_shape=jax.ShapeDtypeStruct((frames, channels, rows, columns), jnp.bfloat16),
        in_specs=[vmem] * 7 + [smem, vmem],
        scratch_shapes=[pltpu.VMEM((frames + 2, rows + 2, channels, columns), jnp.bfloat16)],
    )(
        *lat_frames,
        dk,
        vec,
        upsample_weight,
        mask,
        fk,
    )
    return (latent, rebuilt)


def solution(mesh):
    return jax.shard_map(
        body,
        mesh=mesh,
        in_specs=(P("tm", None, "rows", None), P(), P(), P(), P(), P(), P(), P(), P(), P(), P()),
        out_specs=(P("tm", None, "rows", None), P("tm", None, "rows", None)),
        check_vma=False,
    )
```

```python
import functools

import jax
import jax.numpy as jnp
from jax import lax
from jax.experimental import pallas as pl
from jax.experimental.pallas import tpu as pltpu
from jax.sharding import PartitionSpec as P


def shift(x, dt, dr):
    nt = lax.axis_size("tm")
    nr = lax.axis_size("rows")
    if dt == 0:
        pairs = [(r, r + dr) for r in range(nr) if 0 <= r + dr < nr]
        return lax.ppermute(x, "rows", pairs)
    if dr == 0:
        pairs = [(t, t + dt) for t in range(nt) if 0 <= t + dt < nt]
        return lax.ppermute(x, "tm", pairs)
    pairs = [
        (t * nr + r, (t + dt) * nr + r + dr)
        for t in range(nt)
        for r in range(nr)
        if 0 <= t + dt < nt and 0 <= r + dr < nr
    ]
    return lax.ppermute(x, ("tm", "rows"), pairs)


def merged_kernel(kernel):
    o, c = kernel.shape[3], kernel.shape[4]
    return kernel.transpose(2, 3, 0, 1, 4).reshape(3 * o, 9 * c)


def frame_rows(get, t, r0, rows):
    return jnp.concatenate([get(t, r0 + r) for r in range(rows)], axis=1)


def from_ref(x_ref):
    return lambda t, r: x_ref[t, r]


def tiled(parts, frames_each, rows_top, rows_mid):
    def get(t, r):
        block = parts[t // frames_each]
        f = t % frames_each
        if r < rows_top:
            return block[0][f, r]
        if r < rows_top + rows_mid:
            return block[1][f, r - rows_top]
        return block[2][f, r - rows_top - rows_mid]

    return get


def tap_sum(get, k_ref, t, rows, columns):
    pieces = []
    for a in range(3):
        for b in range(3):
            pieces.append(frame_rows(get, t + a, b, rows))
    stacked = jnp.concatenate(pieces, axis=0)
    acc = jnp.dot(k_ref[...], stacked, preferred_element_type=jnp.float32)
    out_channels = acc.shape[0] // 3
    width = rows * columns
    lane = lax.broadcasted_iota(jnp.int32, (out_channels, width), 1) % columns
    left = pltpu.roll(acc[:out_channels], 1, 1)
    right = pltpu.roll(acc[2 * out_channels :], width - 1, 1)
    left = jnp.where(lane == 0, 0.0, left)
    right = jnp.where(lane == columns - 1, 0.0, right)
    return left + acc[out_channels : 2 * out_channels] + right


def encoder_kernel(
    tc_ref, pv_ref, bc_ref, tp_ref, own_ref, bt_ref,
    k1_ref, vec_ref, mask_ref, k2_ref, w_ref, o_ref, top_ref, bottom_ref, g_ref,
    *, frames, rows, columns
):
    wide = rows + 2
    bias = vec_ref[:, 0:1]
    gain = vec_ref[:, 1:2]
    x = tiled([(tc_ref, pv_ref, bc_ref), (tp_ref, own_ref, bt_ref)], frames, 2, rows)
    for t in range(frames + 2):
        y = tap_sum(x, k1_ref, t, wide, columns) + bias
        scale = lax.rsqrt(jnp.mean(y * y, axis=0, keepdims=True) + 1e-06)
        z = y * scale * gain
        g = z / (1.0 + jnp.exp(-z))
        for r in range(wide):
            piece = g[:, r * columns : (r + 1) * columns] * mask_ref[t, r]
            g_ref[t, r] = piece.astype(g_ref.dtype)
    total = None
    for t in range(frames):
        y = tap_sum(from_ref(g_ref), k2_ref, t, rows, columns)
        res = frame_rows(x, t + frames, 2, rows)
        hidden = (res.astype(jnp.float32) + y).astype(jnp.bfloat16)
        part = jnp.dot(w_ref[t], hidden, preferred_element_type=jnp.float32)
        total = part if total is None else total + part
    for r in range(rows):
        piece = total[:, r * columns : (r + 1) * columns].astype(o_ref.dtype)
        o_ref[0, :, r, :] = piece
        if r < 2:
            bottom_ref[0, :, r, :] = piece
        if r >= rows - 2:
            top_ref[0, :, r - rows + 2, :] = piece


def decode_kernel_body(
    l3_ref, l2_ref, l1_ref, l0_ref, dk_ref, vec_ref, up_ref, mask_ref, fk_ref, o_ref, ext_ref,
    *, frames, rows, columns
):
    wide = rows + 2
    bias = vec_ref[:, 2:3]
    gain = vec_ref[:, 3:4]
    lat_refs = (l3_ref, l2_ref, l1_ref, l0_ref)
    lat = lambda t, r: lat_refs[t][0, :, r, :]
    for f in range(2):
        y = tap_sum(lat, dk_ref, f, wide, columns) + bias
        scale = lax.rsqrt(jnp.mean(y * y, axis=0, keepdims=True) + 1e-06)
        z = y * scale * gain
        act = (z / (1.0 + jnp.exp(-z))).astype(jnp.bfloat16)
        first_j = frames - 2 if f == 0 else 0
        for j in range(first_j, frames):
            up = jnp.dot(up_ref[j], act, preferred_element_type=jnp.float32)
            slot = j - first_j if f == 0 else j + 2
            for r in range(wide):
                piece = up[:, r * columns : (r + 1) * columns] * mask_ref[slot, r]
                ext_ref[slot, r] = piece.astype(ext_ref.dtype)
    for t in range(frames):
        y = tap_sum(from_ref(ext_ref), fk_ref, t, rows, columns)
        res = frame_rows(from_ref(ext_ref), t + 2, 1, rows)
        out = (res.astype(jnp.float32) + y).astype(o_ref.dtype)
        for r in range(rows):
            o_ref[t, :, r, :] = out[:, r * columns : (r + 1) * columns]


def body(
    features,
    first_kernel,
    first_bias,
    first_gain,
    second_kernel,
    latent_weight,
    decode_kernel,
    decode_bias,
    decode_gain,
    upsample_weight,
    final_kernel,
):
    frames, channels, rows, columns = features.shape
    z_count = latent_weight.shape[1]
    dims = dict(frames=frames, rows=rows, columns=columns)
    own = features.transpose(0, 2, 1, 3)
    top = own[:, -2:]
    bottom = own[:, :2]
    previous = shift(own, 1, 0)
    band = lax.axis_index("rows")
    bands = lax.axis_size("rows")
    row_ids = lax.broadcasted_iota(jnp.int32, (frames + 2, rows + 2), 1)
    frame_ids = lax.broadcasted_iota(jnp.int32, (frames + 2, rows + 2), 0)
    inside = ((row_ids > 0) | (band > 0)) & ((row_ids < rows + 1) | (band < bands - 1))
    inside = inside & ((frame_ids >= 2) | (lax.axis_index("tm") > 0))
    params = (
        merged_kernel(first_kernel),
        merged_kernel(second_kernel),
        merged_kernel(decode_kernel),
        merged_kernel(final_kernel),
        jnp.stack([first_bias, first_gain, decode_bias, decode_gain], 1),
        inside.astype(jnp.float32),
    )
    prev_top, prev_bottom, *params = lax.optimization_barrier(
        (previous[:, -2:], previous[:, :2], *params)
    )
    k1, k2, dk, fk, vec, mask = params
    pieces = [
        shift(prev_top, 0, 1),
        previous,
        shift(prev_bottom, 0, -1),
        shift(top, 0, 1),
        own,
        shift(bottom, 0, -1),
    ]
    vmem = pl.BlockSpec(memory_space=pltpu.VMEM)
    smem = pl.BlockSpec(memory_space=pltpu.SMEM)
    latent, lat_top, lat_bottom = pl.pallas_call(
        functools.partial(encoder_kernel, **dims),
        out_shape=(
            jax.ShapeDtypeStruct((1, z_count, rows, columns), jnp.bfloat16),
            jax.ShapeDtypeStruct((1, z_count, 2, columns), jnp.bfloat16),
            jax.ShapeDtypeStruct((1, z_count, 2, columns), jnp.bfloat16),
        ),
        in_specs=[vmem] * 8 + [smem, vmem, vmem],
        scratch_shapes=[pltpu.VMEM((frames + 2, rows + 2, channels, columns), jnp.bfloat16)],
    )(
        *pieces,
        k1,
        vec,
        mask,
        k2,
        latent_weight,
    )
    lat_rows = jnp.concatenate(
        [shift(lat_top, 0, 1), latent, shift(lat_bottom, 0, -1)], 2
    )
    lat_frames = [shift(lat_rows, 3, 0), shift(lat_rows, 2, 0), shift(lat_rows, 1, 0), lat_rows]
    rebuilt = pl.pallas_call(
        functools.partial(decode_kernel_body, **dims),
        out_shape=jax.ShapeDtypeStruct((frames, channels, rows, columns), jnp.bfloat16),
        in_specs=[vmem] * 7 + [smem, vmem],
        scratch_shapes=[pltpu.VMEM((frames + 2, rows + 2, channels, columns), jnp.bfloat16)],
    )(
        *lat_frames,
        dk,
        vec,
        upsample_weight,
        mask,
        fk,
    )
    return (latent, rebuilt)


def solution(mesh):
    return jax.shard_map(
        body,
        mesh=mesh,
        in_specs=(P("tm", None, "rows", None), P(), P(), P(), P(), P(), P(), P(), P(), P(), P()),
        out_specs=(P("tm", None, "rows", None), P("tm", None, "rows", None)),
        check_vma=False,
    )
```

```python
import functools

import jax
import jax.numpy as jnp
from jax import lax
from jax.experimental import pallas as pl
from jax.experimental.pallas import tpu as pltpu
from jax.sharding import PartitionSpec as P


def shift(x, dt, dr):
    nt = lax.axis_size("tm")
    nr = lax.axis_size("rows")
    if dt == 0:
        pairs = [(r, r + dr) for r in range(nr) if 0 <= r + dr < nr]
        return lax.ppermute(x, "rows", pairs)
    if dr == 0:
        pairs = [(t, t + dt) for t in range(nt) if 0 <= t + dt < nt]
        return lax.ppermute(x, "tm", pairs)
    pairs = [
        (t * nr + r, (t + dt) * nr + r + dr)
        for t in range(nt)
        for r in range(nr)
        if 0 <= t + dt < nt and 0 <= r + dr < nr
    ]
    return lax.ppermute(x, ("tm", "rows"), pairs)


def merged_kernel(kernel):
    o, c = kernel.shape[3], kernel.shape[4]
    return kernel.transpose(2, 3, 0, 1, 4).reshape(3 * o, 9 * c)


def frame_rows(get, t, r0, rows):
    return jnp.concatenate([get(t, r0 + r) for r in range(rows)], axis=1)


def from_ref(x_ref):
    return lambda t, r: x_ref[t, r]


def tiled(parts, frames_each, rows_top, rows_mid):
    def get(t, r):
        block = parts[t // frames_each]
        f = t % frames_each
        if r < rows_top:
            return block[0][f, r]
        if r < rows_top + rows_mid:
            return block[1][f, r - rows_top]
        return block[2][f, r - rows_top - rows_mid]

    return get


def tap_sum(get, k_ref, t, rows, columns):
    pieces = []
    for a in range(3):
        for b in range(3):
            pieces.append(frame_rows(get, t + a, b, rows))
    stacked = jnp.concatenate(pieces, axis=0)
    acc = jnp.dot(k_ref[...], stacked, preferred_element_type=jnp.float32)
    out_channels = acc.shape[0] // 3
    width = rows * columns
    lane = lax.broadcasted_iota(jnp.int32, (out_channels, width), 1) % columns
    left = pltpu.roll(acc[:out_channels], 1, 1)
    right = pltpu.roll(acc[2 * out_channels :], width - 1, 1)
    left = jnp.where(lane == 0, 0.0, left)
    right = jnp.where(lane == columns - 1, 0.0, right)
    return left + acc[out_channels : 2 * out_channels] + right


def at_row(get, r):
    return lambda t, rr: get(t, rr + r)


def encoder_kernel(
    tc_ref, pv_ref, bc_ref, tp_ref, own_ref, bt_ref,
    k1_ref, vec_ref, mask_ref, k2_ref, w_ref, o_ref, top_ref, bottom_ref, g_ref,
    *, frames, rows, columns
):
    wide = rows + 2
    bias = vec_ref[:, 0:1]
    gain = vec_ref[:, 1:2]
    x = tiled([(tc_ref, pv_ref, bc_ref), (tp_ref, own_ref, bt_ref)], frames, 2, rows)
    for t in range(frames + 2):
        for r in range(wide):
            y = tap_sum(at_row(x, r), k1_ref, t, 1, columns) + bias
            scale = lax.rsqrt(jnp.mean(y * y, axis=0, keepdims=True) + 1e-06)
            z = y * scale * gain
            g = z / (1.0 + jnp.exp(-z))
            g_ref[t, r] = (g * mask_ref[t, r]).astype(g_ref.dtype)
    totals = [None] * rows
    for t in range(frames):
        for r in range(rows):
            y = tap_sum(at_row(from_ref(g_ref), r), k2_ref, t, 1, columns)
            res = x(t + frames, r + 2)
            hidden = (res.astype(jnp.float32) + y).astype(jnp.bfloat16)
            part = jnp.dot(w_ref[t], hidden, preferred_element_type=jnp.float32)
            totals[r] = part if totals[r] is None else totals[r] + part
    for r in range(rows):
        piece = totals[r].astype(o_ref.dtype)
        o_ref[0, :, r, :] = piece
        if r < 2:
            bottom_ref[0, :, r, :] = piece
        if r >= rows - 2:
            top_ref[0, :, r - rows + 2, :] = piece


def decode_kernel_body(
    l3_ref, l2_ref, l1_ref, l0_ref, dk_ref, vec_ref, up_ref, mask_ref, fk_ref, o_ref, ext_ref,
    *, frames, rows, columns
):
    wide = rows + 2
    bias = vec_ref[:, 2:3]
    gain = vec_ref[:, 3:4]
    lat_refs = (l3_ref, l2_ref, l1_ref, l0_ref)
    lat = lambda t, r: lat_refs[t][0, :, r, :]
    for f in range(2):
        y = tap_sum(lat, dk_ref, f, wide, columns) + bias
        scale = lax.rsqrt(jnp.mean(y * y, axis=0, keepdims=True) + 1e-06)
        z = y * scale * gain
        act = (z / (1.0 + jnp.exp(-z))).astype(jnp.bfloat16)
        first_j = frames - 2 if f == 0 else 0
        for j in range(first_j, frames):
            up = jnp.dot(up_ref[j], act, preferred_element_type=jnp.float32)
            slot = j - first_j if f == 0 else j + 2
            for r in range(wide):
                piece = up[:, r * columns : (r + 1) * columns] * mask_ref[slot, r]
                ext_ref[slot, r] = piece.astype(ext_ref.dtype)
    for t in range(frames):
        for r in range(rows):
            y = tap_sum(at_row(from_ref(ext_ref), r), fk_ref, t, 1, columns)
            res = ext_ref[t + 2, r + 1]
            o_ref[t, :, r, :] = (res.astype(jnp.float32) + y).astype(o_ref.dtype)


def body(
    features,
    first_kernel,
    first_bias,
    first_gain,
    second_kernel,
    latent_weight,
    decode_kernel,
    decode_bias,
    decode_gain,
    upsample_weight,
    final_kernel,
):
    frames, channels, rows, columns = features.shape
    z_count = latent_weight.shape[1]
    dims = dict(frames=frames, rows=rows, columns=columns)
    own = features.transpose(0, 2, 1, 3)
    top = own[:, -2:]
    bottom = own[:, :2]
    previous = shift(own, 1, 0)
    band = lax.axis_index("rows")
    bands = lax.axis_size("rows")
    row_ids = lax.broadcasted_iota(jnp.int32, (frames + 2, rows + 2), 1)
    frame_ids = lax.broadcasted_iota(jnp.int32, (frames + 2, rows + 2), 0)
    inside = ((row_ids > 0) | (band > 0)) & ((row_ids < rows + 1) | (band < bands - 1))
    inside = inside & ((frame_ids >= 2) | (lax.axis_index("tm") > 0))
    params = (
        merged_kernel(first_kernel),
        merged_kernel(second_kernel),
        merged_kernel(decode_kernel),
        merged_kernel(final_kernel),
        jnp.stack([first_bias, first_gain, decode_bias, decode_gain], 1),
        inside.astype(jnp.float32),
    )
    prev_top, prev_bottom, *params = lax.optimization_barrier(
        (previous[:, -2:], previous[:, :2], *params)
    )
    k1, k2, dk, fk, vec, mask = params
    pieces = [
        shift(prev_top, 0, 1),
        previous,
        shift(prev_bottom, 0, -1),
        shift(top, 0, 1),
        own,
        shift(bottom, 0, -1),
    ]
    vmem = pl.BlockSpec(memory_space=pltpu.VMEM)
    smem = pl.BlockSpec(memory_space=pltpu.SMEM)
    latent, lat_top, lat_bottom = pl.pallas_call(
        functools.partial(encoder_kernel, **dims),
        out_shape=(
            jax.ShapeDtypeStruct((1, z_count, rows, columns), jnp.bfloat16),
            jax.ShapeDtypeStruct((1, z_count, 2, columns), jnp.bfloat16),
            jax.ShapeDtypeStruct((1, z_count, 2, columns), jnp.bfloat16),
        ),
        in_specs=[vmem] * 8 + [smem, vmem, vmem],
        scratch_shapes=[pltpu.VMEM((frames + 2, rows + 2, channels, columns), jnp.bfloat16)],
    )(
        *pieces,
        k1,
        vec,
        mask,
        k2,
        latent_weight,
    )
    lat_rows = jnp.concatenate(
        [shift(lat_top, 0, 1), latent, shift(lat_bottom, 0, -1)], 2
    )
    lat_frames = [shift(lat_rows, 3, 0), shift(lat_rows, 2, 0), shift(lat_rows, 1, 0), lat_rows]
    rebuilt = pl.pallas_call(
        functools.partial(decode_kernel_body, **dims),
        out_shape=jax.ShapeDtypeStruct((frames, channels, rows, columns), jnp.bfloat16),
        in_specs=[vmem] * 7 + [smem, vmem],
        scratch_shapes=[pltpu.VMEM((frames + 2, rows + 2, channels, columns), jnp.bfloat16)],
    )(
        *lat_frames,
        dk,
        vec,
        upsample_weight,
        mask,
        fk,
    )
    return (latent, rebuilt)


def solution(mesh):
    return jax.shard_map(
        body,
        mesh=mesh,
        in_specs=(P("tm", None, "rows", None), P(), P(), P(), P(), P(), P(), P(), P(), P(), P()),
        out_specs=(P("tm", None, "rows", None), P("tm", None, "rows", None)),
        check_vma=False,
    )
```

```python
import functools

import jax
import jax.numpy as jnp
from jax import lax
from jax.experimental import pallas as pl
from jax.experimental.pallas import tpu as pltpu
from jax.sharding import PartitionSpec as P


def shift(x, dt, dr):
    nt = lax.axis_size("tm")
    nr = lax.axis_size("rows")
    if dt == 0:
        pairs = [(r, r + dr) for r in range(nr) if 0 <= r + dr < nr]
        return lax.ppermute(x, "rows", pairs)
    if dr == 0:
        pairs = [(t, t + dt) for t in range(nt) if 0 <= t + dt < nt]
        return lax.ppermute(x, "tm", pairs)
    pairs = [
        (t * nr + r, (t + dt) * nr + r + dr)
        for t in range(nt)
        for r in range(nr)
        if 0 <= t + dt < nt and 0 <= r + dr < nr
    ]
    return lax.ppermute(x, ("tm", "rows"), pairs)


def merged_kernel(kernel):
    o, c = kernel.shape[3], kernel.shape[4]
    return kernel.transpose(2, 3, 0, 1, 4).reshape(3 * o, 9 * c)


def frame_rows(get, t, r0, rows):
    return jnp.concatenate([get(t, r0 + r) for r in range(rows)], axis=1)


def from_ref(x_ref):
    return lambda t, r: x_ref[t, r]


def tiled(parts, frames_each, rows_top, rows_mid):
    def get(t, r):
        block = parts[t // frames_each]
        f = t % frames_each
        if r < rows_top:
            return block[0][f, r]
        if r < rows_top + rows_mid:
            return block[1][f, r - rows_top]
        return block[2][f, r - rows_top - rows_mid]

    return get


def tap_sum(get, k_ref, t, rows, columns, count=1):
    pieces = []
    for a in range(3):
        for b in range(3):
            pieces.append(
                jnp.concatenate([frame_rows(get, t + i + a, b, rows) for i in range(count)], axis=1)
            )
    stacked = jnp.concatenate(pieces, axis=0)
    acc = jnp.dot(k_ref[...], stacked, preferred_element_type=jnp.float32)
    out_channels = acc.shape[0] // 3
    width = count * rows * columns
    lane = lax.broadcasted_iota(jnp.int32, (out_channels, width), 1) % columns
    left = pltpu.roll(acc[:out_channels], 1, 1)
    right = pltpu.roll(acc[2 * out_channels :], width - 1, 1)
    left = jnp.where(lane == 0, 0.0, left)
    right = jnp.where(lane == columns - 1, 0.0, right)
    return left + acc[out_channels : 2 * out_channels] + right


def encoder_kernel(
    tc_ref, pv_ref, bc_ref, tp_ref, own_ref, bt_ref,
    k1_ref, vec_ref, mask_ref, k2_ref, w_ref, o_ref, top_ref, bottom_ref, g_ref,
    *, frames, rows, columns
):
    wide = rows + 2
    bias = vec_ref[:, 0:1]
    gain = vec_ref[:, 1:2]
    x = tiled([(tc_ref, pv_ref, bc_ref), (tp_ref, own_ref, bt_ref)], frames, 2, rows)
    span = wide * columns
    for t in range(0, frames + 2, 2):
        y = tap_sum(x, k1_ref, t, wide, columns, 2) + bias
        scale = lax.rsqrt(jnp.mean(y * y, axis=0, keepdims=True) + 1e-06)
        z = y * scale * gain
        g = z / (1.0 + jnp.exp(-z))
        for i in range(2):
            for r in range(wide):
                lo = i * span + r * columns
                piece = g[:, lo : lo + columns] * mask_ref[t + i, r]
                g_ref[t + i, r] = piece.astype(g_ref.dtype)
    total = None
    width = rows * columns
    for t in range(0, frames, 2):
        y = tap_sum(from_ref(g_ref), k2_ref, t, rows, columns, 2)
        for i in range(2):
            res = frame_rows(x, t + i + frames, 2, rows)
            hidden = (res.astype(jnp.float32) + y[:, i * width : (i + 1) * width]).astype(jnp.bfloat16)
            part = jnp.dot(w_ref[t + i], hidden, preferred_element_type=jnp.float32)
            total = part if total is None else total + part
    for r in range(rows):
        piece = total[:, r * columns : (r + 1) * columns].astype(o_ref.dtype)
        o_ref[0, :, r, :] = piece
        if r < 2:
            bottom_ref[0, :, r, :] = piece
        if r >= rows - 2:
            top_ref[0, :, r - rows + 2, :] = piece


def decode_kernel_body(
    l3_ref, l2_ref, l1_ref, l0_ref, dk_ref, vec_ref, up_ref, mask_ref, fk_ref, o_ref, ext_ref,
    *, frames, rows, columns
):
    wide = rows + 2
    bias = vec_ref[:, 2:3]
    gain = vec_ref[:, 3:4]
    lat_refs = (l3_ref, l2_ref, l1_ref, l0_ref)
    lat = lambda t, r: lat_refs[t][0, :, r, :]
    for f in range(2):
        y = tap_sum(lat, dk_ref, f, wide, columns) + bias
        scale = lax.rsqrt(jnp.mean(y * y, axis=0, keepdims=True) + 1e-06)
        z = y * scale * gain
        act = (z / (1.0 + jnp.exp(-z))).astype(jnp.bfloat16)
        first_j = frames - 2 if f == 0 else 0
        for j in range(first_j, frames):
            up = jnp.dot(up_ref[j], act, preferred_element_type=jnp.float32)
            slot = j - first_j if f == 0 else j + 2
            for r in range(wide):
                piece = up[:, r * columns : (r + 1) * columns] * mask_ref[slot, r]
                ext_ref[slot, r] = piece.astype(ext_ref.dtype)
    for t in range(frames):
        y = tap_sum(from_ref(ext_ref), fk_ref, t, rows, columns)
        res = frame_rows(from_ref(ext_ref), t + 2, 1, rows)
        out = (res.astype(jnp.float32) + y).astype(o_ref.dtype)
        for r in range(rows):
            o_ref[t, :, r, :] = out[:, r * columns : (r + 1) * columns]


def body(
    features,
    first_kernel,
    first_bias,
    first_gain,
    second_kernel,
    latent_weight,
    decode_kernel,
    decode_bias,
    decode_gain,
    upsample_weight,
    final_kernel,
):
    frames, channels, rows, columns = features.shape
    z_count = latent_weight.shape[1]
    dims = dict(frames=frames, rows=rows, columns=columns)
    own = features.transpose(0, 2, 1, 3)
    top = own[:, -2:]
    bottom = own[:, :2]
    previous = shift(own, 1, 0)
    band = lax.axis_index("rows")
    bands = lax.axis_size("rows")
    row_ids = lax.broadcasted_iota(jnp.int32, (frames + 2, rows + 2), 1)
    frame_ids = lax.broadcasted_iota(jnp.int32, (frames + 2, rows + 2), 0)
    inside = ((row_ids > 0) | (band > 0)) & ((row_ids < rows + 1) | (band < bands - 1))
    inside = inside & ((frame_ids >= 2) | (lax.axis_index("tm") > 0))
    params = (
        merged_kernel(first_kernel),
        merged_kernel(second_kernel),
        merged_kernel(decode_kernel),
        merged_kernel(final_kernel),
        jnp.stack([first_bias, first_gain, decode_bias, decode_gain], 1),
        inside.astype(jnp.float32),
    )
    prev_top, prev_bottom, *params = lax.optimization_barrier(
        (previous[:, -2:], previous[:, :2], *params)
    )
    k1, k2, dk, fk, vec, mask = params
    pieces = [
        shift(prev_top, 0, 1),
        previous,
        shift(prev_bottom, 0, -1),
        shift(top, 0, 1),
        own,
        shift(bottom, 0, -1),
    ]
    vmem = pl.BlockSpec(memory_space=pltpu.VMEM)
    smem = pl.BlockSpec(memory_space=pltpu.SMEM)
    latent, lat_top, lat_bottom = pl.pallas_call(
        functools.partial(encoder_kernel, **dims),
        out_shape=(
            jax.ShapeDtypeStruct((1, z_count, rows, columns), jnp.bfloat16),
            jax.ShapeDtypeStruct((1, z_count, 2, columns), jnp.bfloat16),
            jax.ShapeDtypeStruct((1, z_count, 2, columns), jnp.bfloat16),
        ),
        in_specs=[vmem] * 8 + [smem, vmem, vmem],
        scratch_shapes=[pltpu.VMEM((frames + 2, rows + 2, channels, columns), jnp.bfloat16)],
    )(
        *pieces,
        k1,
        vec,
        mask,
        k2,
        latent_weight,
    )
    lat_rows = jnp.concatenate(
        [shift(lat_top, 0, 1), latent, shift(lat_bottom, 0, -1)], 2
    )
    lat_frames = [shift(lat_rows, 3, 0), shift(lat_rows, 2, 0), shift(lat_rows, 1, 0), lat_rows]
    rebuilt = pl.pallas_call(
        functools.partial(decode_kernel_body, **dims),
        out_shape=jax.ShapeDtypeStruct((frames, channels, rows, columns), jnp.bfloat16),
        in_specs=[vmem] * 7 + [smem, vmem],
        scratch_shapes=[pltpu.VMEM((frames + 2, rows + 2, channels, columns), jnp.bfloat16)],
    )(
        *lat_frames,
        dk,
        vec,
        upsample_weight,
        mask,
        fk,
    )
    return (latent, rebuilt)


def solution(mesh):
    return jax.shard_map(
        body,
        mesh=mesh,
        in_specs=(P("tm", None, "rows", None), P(), P(), P(), P(), P(), P(), P(), P(), P(), P()),
        out_specs=(P("tm", None, "rows", None), P("tm", None, "rows", None)),
        check_vma=False,
    )
```

```python
import functools

import jax
import jax.numpy as jnp
from jax import lax
from jax.experimental import pallas as pl
from jax.experimental.pallas import tpu as pltpu
from jax.sharding import PartitionSpec as P


def shift(x, dt, dr):
    nt = lax.axis_size("tm")
    nr = lax.axis_size("rows")
    if dt == 0:
        pairs = [(r, r + dr) for r in range(nr) if 0 <= r + dr < nr]
        return lax.ppermute(x, "rows", pairs)
    if dr == 0:
        pairs = [(t, t + dt) for t in range(nt) if 0 <= t + dt < nt]
        return lax.ppermute(x, "tm", pairs)
    pairs = [
        (t * nr + r, (t + dt) * nr + r + dr)
        for t in range(nt)
        for r in range(nr)
        if 0 <= t + dt < nt and 0 <= r + dr < nr
    ]
    return lax.ppermute(x, ("tm", "rows"), pairs)


def merged_kernel(kernel):
    o, c = kernel.shape[3], kernel.shape[4]
    return kernel.transpose(2, 3, 0, 1, 4).reshape(3 * o, 9 * c)


def frame_rows(get, t, r0, rows):
    return jnp.concatenate([get(t, r0 + r) for r in range(rows)], axis=1)


def from_ref(x_ref):
    return lambda t, r: x_ref[t, r]


def tiled(parts, frames_each, rows_top, rows_mid):
    def get(t, r):
        block = parts[t // frames_each]
        f = t % frames_each
        if r < rows_top:
            return block[0][f, r]
        if r < rows_top + rows_mid:
            return block[1][f, r - rows_top]
        return block[2][f, r - rows_top - rows_mid]

    return get


def tap_sum(get, k_ref, t, rows, columns, count=1):
    pieces = []
    for a in range(3):
        for b in range(3):
            pieces.append(
                jnp.concatenate([frame_rows(get, t + i + a, b, rows) for i in range(count)], axis=1)
            )
    stacked = jnp.concatenate(pieces, axis=0)
    acc = jnp.dot(k_ref[...], stacked, preferred_element_type=jnp.float32)
    out_channels = acc.shape[0] // 3
    width = count * rows * columns
    lane = lax.broadcasted_iota(jnp.int32, (out_channels, width), 1) % columns
    left = pltpu.roll(acc[:out_channels], 1, 1)
    right = pltpu.roll(acc[2 * out_channels :], width - 1, 1)
    left = jnp.where(lane == 0, 0.0, left)
    right = jnp.where(lane == columns - 1, 0.0, right)
    return left + acc[out_channels : 2 * out_channels] + right


def late_gate_kernel(
    tp_ref, own_ref, bt_ref, k1_ref, vec_ref, mask_ref, o_ref, *, frames, rows, columns
):
    wide = rows + 2
    span = wide * columns
    x = tiled([(tp_ref, own_ref, bt_ref)], frames, 2, rows)
    y = tap_sum(x, k1_ref, frames - 4, wide, columns, 2) + vec_ref[:, 0:1]
    scale = lax.rsqrt(jnp.mean(y * y, axis=0, keepdims=True) + 1e-06)
    z = y * scale * vec_ref[:, 1:2]
    g = z / (1.0 + jnp.exp(-z))
    for i in range(2):
        for r in range(wide):
            lo = i * span + r * columns
            piece = g[:, lo : lo + columns] * mask_ref[frames + i, r]
            o_ref[i, r] = piece.astype(o_ref.dtype)


def encoder_kernel(
    tc_ref, pv_ref, bc_ref, tp_ref, own_ref, bt_ref, late_ref,
    k1_ref, vec_ref, mask_ref, k2_ref, w_ref, o_ref, top_ref, bottom_ref, g_ref,
    *, frames, rows, columns
):
    wide = rows + 2
    bias = vec_ref[:, 0:1]
    gain = vec_ref[:, 1:2]
    x = tiled([(tc_ref, pv_ref, bc_ref), (tp_ref, own_ref, bt_ref)], frames, 2, rows)
    span = wide * columns
    for t in range(0, frames, 2):
        y = tap_sum(x, k1_ref, t, wide, columns, 2) + bias
        scale = lax.rsqrt(jnp.mean(y * y, axis=0, keepdims=True) + 1e-06)
        z = y * scale * gain
        g = z / (1.0 + jnp.exp(-z))
        for i in range(2):
            for r in range(wide):
                lo = i * span + r * columns
                piece = g[:, lo : lo + columns] * mask_ref[t + i, r]
                g_ref[t + i, r] = piece.astype(g_ref.dtype)
    gated = lambda t, r: g_ref[t, r] if t < frames else late_ref[t - frames, r]
    total = None
    width = rows * columns
    for t in range(0, frames, 2):
        y = tap_sum(gated, k2_ref, t, rows, columns, 2)
        for i in range(2):
            res = frame_rows(x, t + i + frames, 2, rows)
            hidden = (res.astype(jnp.float32) + y[:, i * width : (i + 1) * width]).astype(jnp.bfloat16)
            part = jnp.dot(w_ref[t + i], hidden, preferred_element_type=jnp.float32)
            total = part if total is None else total + part
    for r in range(rows):
        piece = total[:, r * columns : (r + 1) * columns].astype(o_ref.dtype)
        o_ref[0, :, r, :] = piece
        if r < 2:
            bottom_ref[0, :, r, :] = piece
        if r >= rows - 2:
            top_ref[0, :, r - rows + 2, :] = piece


def decode_kernel_body(
    l3_ref, l2_ref, l1_ref, l0_ref, dk_ref, vec_ref, up_ref, mask_ref, fk_ref, o_ref, ext_ref,
    *, frames, rows, columns
):
    wide = rows + 2
    bias = vec_ref[:, 2:3]
    gain = vec_ref[:, 3:4]
    lat_refs = (l3_ref, l2_ref, l1_ref, l0_ref)
    lat = lambda t, r: lat_refs[t][0, :, r, :]
    for f in range(2):
        y = tap_sum(lat, dk_ref, f, wide, columns) + bias
        scale = lax.rsqrt(jnp.mean(y * y, axis=0, keepdims=True) + 1e-06)
        z = y * scale * gain
        act = (z / (1.0 + jnp.exp(-z))).astype(jnp.bfloat16)
        first_j = frames - 2 if f == 0 else 0
        for j in range(first_j, frames):
            up = jnp.dot(up_ref[j], act, preferred_element_type=jnp.float32)
            slot = j - first_j if f == 0 else j + 2
            for r in range(wide):
                piece = up[:, r * columns : (r + 1) * columns] * mask_ref[slot, r]
                ext_ref[slot, r] = piece.astype(ext_ref.dtype)
    for t in range(frames):
        y = tap_sum(from_ref(ext_ref), fk_ref, t, rows, columns)
        res = frame_rows(from_ref(ext_ref), t + 2, 1, rows)
        out = (res.astype(jnp.float32) + y).astype(o_ref.dtype)
        for r in range(rows):
            o_ref[t, :, r, :] = out[:, r * columns : (r + 1) * columns]


def body(
    features,
    first_kernel,
    first_bias,
    first_gain,
    second_kernel,
    latent_weight,
    decode_kernel,
    decode_bias,
    decode_gain,
    upsample_weight,
    final_kernel,
):
    frames, channels, rows, columns = features.shape
    z_count = latent_weight.shape[1]
    dims = dict(frames=frames, rows=rows, columns=columns)
    own = features.transpose(0, 2, 1, 3)
    top = own[:, -2:]
    bottom = own[:, :2]
    previous = shift(own, 1, 0)
    band = lax.axis_index("rows")
    bands = lax.axis_size("rows")
    row_ids = lax.broadcasted_iota(jnp.int32, (frames + 2, rows + 2), 1)
    frame_ids = lax.broadcasted_iota(jnp.int32, (frames + 2, rows + 2), 0)
    inside = ((row_ids > 0) | (band > 0)) & ((row_ids < rows + 1) | (band < bands - 1))
    inside = inside & ((frame_ids >= 2) | (lax.axis_index("tm") > 0))
    params = (
        merged_kernel(first_kernel),
        merged_kernel(second_kernel),
        merged_kernel(decode_kernel),
        merged_kernel(final_kernel),
        jnp.stack([first_bias, first_gain, decode_bias, decode_gain], 1),
        inside.astype(jnp.float32),
    )
    prev_top, prev_bottom, *params = lax.optimization_barrier(
        (previous[:, -2:], previous[:, :2], *params)
    )
    k1, k2, dk, fk, vec, mask = params
    pieces = [
        shift(prev_top, 0, 1),
        previous,
        shift(prev_bottom, 0, -1),
        shift(top, 0, 1),
        own,
        shift(bottom, 0, -1),
    ]
    vmem = pl.BlockSpec(memory_space=pltpu.VMEM)
    smem = pl.BlockSpec(memory_space=pltpu.SMEM)
    late = pl.pallas_call(
        functools.partial(late_gate_kernel, **dims),
        out_shape=jax.ShapeDtypeStruct((2, rows + 2, channels, columns), jnp.bfloat16),
        in_specs=[vmem] * 5 + [smem],
    )(pieces[3], own, pieces[5], k1, vec, mask)
    latent, lat_top, lat_bottom = pl.pallas_call(
        functools.partial(encoder_kernel, **dims),
        out_shape=(
            jax.ShapeDtypeStruct((1, z_count, rows, columns), jnp.bfloat16),
            jax.ShapeDtypeStruct((1, z_count, 2, columns), jnp.bfloat16),
            jax.ShapeDtypeStruct((1, z_count, 2, columns), jnp.bfloat16),
        ),
        in_specs=[vmem] * 9 + [smem, vmem, vmem],
        scratch_shapes=[pltpu.VMEM((frames, rows + 2, channels, columns), jnp.bfloat16)],
    )(
        *pieces,
        late,
        k1,
        vec,
        mask,
        k2,
        latent_weight,
    )
    lat_rows = jnp.concatenate(
        [shift(lat_top, 0, 1), latent, shift(lat_bottom, 0, -1)], 2
    )
    lat_frames = [shift(lat_rows, 3, 0), shift(lat_rows, 2, 0), shift(lat_rows, 1, 0), lat_rows]
    rebuilt = pl.pallas_call(
        functools.partial(decode_kernel_body, **dims),
        out_shape=jax.ShapeDtypeStruct((frames, channels, rows, columns), jnp.bfloat16),
        in_specs=[vmem] * 7 + [smem, vmem],
        scratch_shapes=[pltpu.VMEM((frames + 2, rows + 2, channels, columns), jnp.bfloat16)],
    )(
        *lat_frames,
        dk,
        vec,
        upsample_weight,
        mask,
        fk,
    )
    return (latent, rebuilt)


def solution(mesh):
    return jax.shard_map(
        body,
        mesh=mesh,
        in_specs=(P("tm", None, "rows", None), P(), P(), P(), P(), P(), P(), P(), P(), P(), P()),
        out_specs=(P("tm", None, "rows", None), P("tm", None, "rows", None)),
        check_vma=False,
    )
```

```python
import functools

import jax
import jax.numpy as jnp
from jax import lax
from jax.experimental import pallas as pl
from jax.experimental.pallas import tpu as pltpu
from jax.sharding import PartitionSpec as P


def shift(x, dt, dr):
    nt = lax.axis_size("tm")
    nr = lax.axis_size("rows")
    if dt == 0:
        pairs = [(r, r + dr) for r in range(nr) if 0 <= r + dr < nr]
        return lax.ppermute(x, "rows", pairs)
    if dr == 0:
        pairs = [(t, t + dt) for t in range(nt) if 0 <= t + dt < nt]
        return lax.ppermute(x, "tm", pairs)
    pairs = [
        (t * nr + r, (t + dt) * nr + r + dr)
        for t in range(nt)
        for r in range(nr)
        if 0 <= t + dt < nt and 0 <= r + dr < nr
    ]
    return lax.ppermute(x, ("tm", "rows"), pairs)


def merged_kernel(kernel):
    o, c = kernel.shape[3], kernel.shape[4]
    return kernel.transpose(2, 3, 0, 1, 4).reshape(3 * o, 9 * c)


def frame_rows(get, t, r0, rows):
    return jnp.concatenate([get(t, r0 + r) for r in range(rows)], axis=1)


def from_ref(x_ref):
    return lambda t, r: x_ref[t, r]


def tiled(parts, frames_each, rows_top, rows_mid):
    def get(t, r):
        block = parts[t // frames_each]
        f = t % frames_each
        if r < rows_top:
            return block[0][f, r]
        if r < rows_top + rows_mid:
            return block[1][f, r - rows_top]
        return block[2][f, r - rows_top - rows_mid]

    return get


def tap_sum(get, k_ref, t, rows, columns, count=1):
    pieces = []
    for a in range(3):
        for b in range(3):
            pieces.append(
                jnp.concatenate([frame_rows(get, t + i + a, b, rows) for i in range(count)], axis=1)
            )
    stacked = jnp.concatenate(pieces, axis=0)
    acc = jnp.dot(k_ref[...], stacked, preferred_element_type=jnp.float32)
    out_channels = acc.shape[0] // 3
    width = count * rows * columns
    lane = lax.broadcasted_iota(jnp.int32, (out_channels, width), 1) % columns
    left = pltpu.roll(acc[:out_channels], 1, 1)
    right = pltpu.roll(acc[2 * out_channels :], width - 1, 1)
    left = jnp.where(lane == 0, 0.0, left)
    right = jnp.where(lane == columns - 1, 0.0, right)
    return left + acc[out_channels : 2 * out_channels] + right


def at_row(get, r):
    return lambda t, rr: get(t, rr + r)


def gate_block(x, k1_ref, vec_ref, mask_ref, t, r0, count, columns, store):
    span = count * columns
    y = tap_sum(at_row(x, r0), k1_ref, t, count, columns, 2) + vec_ref[:, 0:1]
    scale = lax.rsqrt(jnp.mean(y * y, axis=0, keepdims=True) + 1e-06)
    z = y * scale * vec_ref[:, 1:2]
    g = z / (1.0 + jnp.exp(-z))
    for i in range(2):
        for r in range(count):
            lo = i * span + r * columns
            store(i, r, g[:, lo : lo + columns])


def late_gate_kernel(
    tp_ref, own_ref, bt_ref, k1_ref, vec_ref, mask_ref, o_ref, *, frames, rows, columns
):
    x = tiled([(tp_ref, own_ref, bt_ref)], frames, 2, rows)

    def store(i, r, piece):
        o_ref[i, r] = (piece * mask_ref[frames + i, r]).astype(o_ref.dtype)

    gate_block(x, k1_ref, vec_ref, mask_ref, frames - 4, 0, rows + 2, columns, store)


def inner_gate_kernel(pv_ref, own_ref, k1_ref, vec_ref, mask_ref, o_ref, *, frames, rows, columns):
    x = tiled([(None, pv_ref, None), (None, own_ref, None)], frames, 2, rows)
    for t in range(0, frames, 2):

        def store(i, r, piece, t=t):
            o_ref[t + i, r] = (piece * mask_ref[t + i, r + 2]).astype(o_ref.dtype)

        gate_block(x, k1_ref, vec_ref, mask_ref, t, 2, rows - 2, columns, store)


def encoder_kernel(
    tc_ref, pv_ref, bc_ref, tp_ref, own_ref, bt_ref, late_ref, inner_ref,
    k1_ref, vec_ref, mask_ref, k2_ref, w_ref, o_ref, top_ref, bottom_ref, g_ref,
    *, frames, rows, columns
):
    x = tiled([(tc_ref, pv_ref, bc_ref), (tp_ref, own_ref, bt_ref)], frames, 2, rows)
    for t in range(0, frames, 2):
        for r0 in (0, rows):

            def store(i, r, piece, t=t, r0=r0):
                g_ref[t + i, r0 + r] = (piece * mask_ref[t + i, r0 + r]).astype(g_ref.dtype)

            gate_block(x, k1_ref, vec_ref, mask_ref, t, r0, 2, columns, store)

    def gated(t, r):
        if t >= frames:
            return late_ref[t - frames, r]
        if 2 <= r < rows:
            return inner_ref[t, r - 2]
        return g_ref[t, r]

    total = None
    width = rows * columns
    for t in range(0, frames, 2):
        y = tap_sum(gated, k2_ref, t, rows, columns, 2)
        for i in range(2):
            res = frame_rows(x, t + i + frames, 2, rows)
            hidden = (res.astype(jnp.float32) + y[:, i * width : (i + 1) * width]).astype(jnp.bfloat16)
            part = jnp.dot(w_ref[t + i], hidden, preferred_element_type=jnp.float32)
            total = part if total is None else total + part
    for r in range(rows):
        piece = total[:, r * columns : (r + 1) * columns].astype(o_ref.dtype)
        o_ref[0, :, r, :] = piece
        if r < 2:
            bottom_ref[0, :, r, :] = piece
        if r >= rows - 2:
            top_ref[0, :, r - rows + 2, :] = piece


def decode_kernel_body(
    l3_ref, l2_ref, l1_ref, l0_ref, dk_ref, vec_ref, up_ref, mask_ref, fk_ref, o_ref, ext_ref,
    *, frames, rows, columns
):
    wide = rows + 2
    bias = vec_ref[:, 2:3]
    gain = vec_ref[:, 3:4]
    lat_refs = (l3_ref, l2_ref, l1_ref, l0_ref)
    lat = lambda t, r: lat_refs[t][0, :, r, :]
    for f in range(2):
        y = tap_sum(lat, dk_ref, f, wide, columns) + bias
        scale = lax.rsqrt(jnp.mean(y * y, axis=0, keepdims=True) + 1e-06)
        z = y * scale * gain
        act = (z / (1.0 + jnp.exp(-z))).astype(jnp.bfloat16)
        first_j = frames - 2 if f == 0 else 0
        for j in range(first_j, frames):
            up = jnp.dot(up_ref[j], act, preferred_element_type=jnp.float32)
            slot = j - first_j if f == 0 else j + 2
            for r in range(wide):
                piece = up[:, r * columns : (r + 1) * columns] * mask_ref[slot, r]
                ext_ref[slot, r] = piece.astype(ext_ref.dtype)
    for t in range(frames):
        y = tap_sum(from_ref(ext_ref), fk_ref, t, rows, columns)
        res = frame_rows(from_ref(ext_ref), t + 2, 1, rows)
        out = (res.astype(jnp.float32) + y).astype(o_ref.dtype)
        for r in range(rows):
            o_ref[t, :, r, :] = out[:, r * columns : (r + 1) * columns]


def body(
    features,
    first_kernel,
    first_bias,
    first_gain,
    second_kernel,
    latent_weight,
    decode_kernel,
    decode_bias,
    decode_gain,
    upsample_weight,
    final_kernel,
):
    frames, channels, rows, columns = features.shape
    z_count = latent_weight.shape[1]
    dims = dict(frames=frames, rows=rows, columns=columns)
    own = features.transpose(0, 2, 1, 3)
    top = own[:, -2:]
    bottom = own[:, :2]
    previous = shift(own, 1, 0)
    band = lax.axis_index("rows")
    bands = lax.axis_size("rows")
    row_ids = lax.broadcasted_iota(jnp.int32, (frames + 2, rows + 2), 1)
    frame_ids = lax.broadcasted_iota(jnp.int32, (frames + 2, rows + 2), 0)
    inside = ((row_ids > 0) | (band > 0)) & ((row_ids < rows + 1) | (band < bands - 1))
    inside = inside & ((frame_ids >= 2) | (lax.axis_index("tm") > 0))
    params = (
        merged_kernel(first_kernel),
        merged_kernel(second_kernel),
        merged_kernel(decode_kernel),
        merged_kernel(final_kernel),
        jnp.stack([first_bias, first_gain, decode_bias, decode_gain], 1),
        inside.astype(jnp.float32),
    )
    prev_top, prev_bottom, *params = lax.optimization_barrier(
        (previous[:, -2:], previous[:, :2], *params)
    )
    k1, k2, dk, fk, vec, mask = params
    pieces = [
        shift(prev_top, 0, 1),
        previous,
        shift(prev_bottom, 0, -1),
        shift(top, 0, 1),
        own,
        shift(bottom, 0, -1),
    ]
    vmem = pl.BlockSpec(memory_space=pltpu.VMEM)
    smem = pl.BlockSpec(memory_space=pltpu.SMEM)
    late = pl.pallas_call(
        functools.partial(late_gate_kernel, **dims),
        out_shape=jax.ShapeDtypeStruct((2, rows + 2, channels, columns), jnp.bfloat16),
        in_specs=[vmem] * 5 + [smem],
    )(pieces[3], own, pieces[5], k1, vec, mask)
    inner = pl.pallas_call(
        functools.partial(inner_gate_kernel, **dims),
        out_shape=jax.ShapeDtypeStruct((frames, rows - 2, channels, columns), jnp.bfloat16),
        in_specs=[vmem] * 4 + [smem],
    )(previous, own, k1, vec, mask)
    latent, lat_top, lat_bottom = pl.pallas_call(
        functools.partial(encoder_kernel, **dims),
        out_shape=(
            jax.ShapeDtypeStruct((1, z_count, rows, columns), jnp.bfloat16),
            jax.ShapeDtypeStruct((1, z_count, 2, columns), jnp.bfloat16),
            jax.ShapeDtypeStruct((1, z_count, 2, columns), jnp.bfloat16),
        ),
        in_specs=[vmem] * 10 + [smem, vmem, vmem],
        scratch_shapes=[pltpu.VMEM((frames, rows + 2, channels, columns), jnp.bfloat16)],
    )(
        *pieces,
        late,
        inner,
        k1,
        vec,
        mask,
        k2,
        latent_weight,
    )
    lat_rows = jnp.concatenate(
        [shift(lat_top, 0, 1), latent, shift(lat_bottom, 0, -1)], 2
    )
    lat_frames = [shift(lat_rows, 3, 0), shift(lat_rows, 2, 0), shift(lat_rows, 1, 0), lat_rows]
    rebuilt = pl.pallas_call(
        functools.partial(decode_kernel_body, **dims),
        out_shape=jax.ShapeDtypeStruct((frames, channels, rows, columns), jnp.bfloat16),
        in_specs=[vmem] * 7 + [smem, vmem],
        scratch_shapes=[pltpu.VMEM((frames + 2, rows + 2, channels, columns), jnp.bfloat16)],
    )(
        *lat_frames,
        dk,
        vec,
        upsample_weight,
        mask,
        fk,
    )
    return (latent, rebuilt)


def solution(mesh):
    return jax.shard_map(
        body,
        mesh=mesh,
        in_specs=(P("tm", None, "rows", None), P(), P(), P(), P(), P(), P(), P(), P(), P(), P()),
        out_specs=(P("tm", None, "rows", None), P("tm", None, "rows", None)),
        check_vma=False,
    )
```

```python
import functools

import jax
import jax.numpy as jnp
from jax import lax
from jax.experimental import pallas as pl
from jax.experimental.pallas import tpu as pltpu
from jax.sharding import PartitionSpec as P


def shift(x, dt, dr):
    nt = lax.axis_size("tm")
    nr = lax.axis_size("rows")
    if dt == 0:
        pairs = [(r, r + dr) for r in range(nr) if 0 <= r + dr < nr]
        return lax.ppermute(x, "rows", pairs)
    if dr == 0:
        pairs = [(t, t + dt) for t in range(nt) if 0 <= t + dt < nt]
        return lax.ppermute(x, "tm", pairs)
    pairs = [
        (t * nr + r, (t + dt) * nr + r + dr)
        for t in range(nt)
        for r in range(nr)
        if 0 <= t + dt < nt and 0 <= r + dr < nr
    ]
    return lax.ppermute(x, ("tm", "rows"), pairs)


def merged_kernel(kernel):
    o, c = kernel.shape[3], kernel.shape[4]
    return kernel.transpose(2, 3, 0, 1, 4).reshape(3 * o, 9 * c)


def frame_rows(get, t, r0, rows):
    return jnp.concatenate([get(t, r0 + r) for r in range(rows)], axis=1)


def from_ref(x_ref):
    return lambda t, r: x_ref[t, r]


def tiled(parts, frames_each, rows_top, rows_mid):
    def get(t, r):
        block = parts[t // frames_each]
        f = t % frames_each
        if r < rows_top:
            return block[0][f, r]
        if r < rows_top + rows_mid:
            return block[1][f, r - rows_top]
        return block[2][f, r - rows_top - rows_mid]

    return get


def tap_sum(get, k_ref, t, rows, columns, count=1):
    pieces = []
    for a in range(3):
        for b in range(3):
            pieces.append(
                jnp.concatenate([frame_rows(get, t + i + a, b, rows) for i in range(count)], axis=1)
            )
    stacked = jnp.concatenate(pieces, axis=0)
    acc = jnp.dot(k_ref[...], stacked, preferred_element_type=jnp.float32)
    out_channels = acc.shape[0] // 3
    width = count * rows * columns
    lane = lax.broadcasted_iota(jnp.int32, (out_channels, width), 1) % columns
    left = pltpu.roll(acc[:out_channels], 1, 1)
    right = pltpu.roll(acc[2 * out_channels :], width - 1, 1)
    left = jnp.where(lane == 0, 0.0, left)
    right = jnp.where(lane == columns - 1, 0.0, right)
    return left + acc[out_channels : 2 * out_channels] + right


def late_gate_kernel(
    tp_ref, own_ref, bt_ref, k1_ref, vec_ref, mask_ref, o_ref, *, frames, rows, columns
):
    wide = rows + 2
    span = wide * columns
    x = tiled([(tp_ref, own_ref, bt_ref)], frames, 2, rows)
    y = tap_sum(x, k1_ref, frames - 4, wide, columns, 2) + vec_ref[:, 0:1]
    scale = lax.rsqrt(jnp.mean(y * y, axis=0, keepdims=True) + 1e-06)
    z = y * scale * vec_ref[:, 1:2]
    g = z / (1.0 + jnp.exp(-z))
    for i in range(2):
        for r in range(wide):
            lo = i * span + r * columns
            piece = g[:, lo : lo + columns] * mask_ref[frames + i, r]
            o_ref[i, r] = piece.astype(o_ref.dtype)


def encoder_kernel(
    tc_ref, pv_ref, bc_ref, tp_ref, own_ref, bt_ref, late_ref,
    k1_ref, vec_ref, mask_ref, k2_ref, w_ref, o_ref, top_ref, bottom_ref, g_ref,
    *, frames, rows, columns
):
    wide = rows + 2
    bias = vec_ref[:, 0:1]
    gain = vec_ref[:, 1:2]
    x = tiled([(tc_ref, pv_ref, bc_ref), (tp_ref, own_ref, bt_ref)], frames, 2, rows)
    span = wide * columns
    for t in range(0, frames, 2):
        y = tap_sum(x, k1_ref, t, wide, columns, 2) + bias
        scale = lax.rsqrt(jnp.mean(y * y, axis=0, keepdims=True) + 1e-06)
        z = y * scale * gain
        g = z / (1.0 + jnp.exp(-z))
        for i in range(2):
            for r in range(wide):
                lo = i * span + r * columns
                piece = g[:, lo : lo + columns] * mask_ref[t + i, r]
                g_ref[t + i, r] = piece.astype(g_ref.dtype)
    gated = lambda t, r: g_ref[t, r] if t < frames else late_ref[t - frames, r]
    total = None
    width = rows * columns
    for t in range(0, frames, 2):
        y = tap_sum(gated, k2_ref, t, rows, columns, 2)
        for i in range(2):
            res = frame_rows(x, t + i + frames, 2, rows)
            hidden = (res.astype(jnp.float32) + y[:, i * width : (i + 1) * width]).astype(jnp.bfloat16)
            part = jnp.dot(w_ref[t + i], hidden, preferred_element_type=jnp.float32)
            total = part if total is None else total + part
    for r in range(rows):
        piece = total[:, r * columns : (r + 1) * columns].astype(o_ref.dtype)
        o_ref[0, :, r, :] = piece
        if r < 2:
            bottom_ref[0, :, r, :] = piece
        if r >= rows - 2:
            top_ref[0, :, r - rows + 2, :] = piece


def decode_kernel_body(
    l3_ref, l2_ref, l1_ref, l0_ref, dk_ref, vec_ref, up_ref, mask_ref, fk_ref, o_ref, ext_ref,
    *, frames, rows, columns
):
    wide = rows + 2
    bias = vec_ref[:, 2:3]
    gain = vec_ref[:, 3:4]
    lat_refs = (l3_ref, l2_ref, l1_ref, l0_ref)
    lat = lambda t, r: lat_refs[t][0, :, r, :]
    for f in range(2):
        y = tap_sum(lat, dk_ref, f, wide, columns) + bias
        scale = lax.rsqrt(jnp.mean(y * y, axis=0, keepdims=True) + 1e-06)
        z = y * scale * gain
        act = (z / (1.0 + jnp.exp(-z))).astype(jnp.bfloat16)
        first_j = frames - 2 if f == 0 else 0
        for j in range(first_j, frames):
            up = jnp.dot(up_ref[j], act, preferred_element_type=jnp.float32)
            slot = j - first_j if f == 0 else j + 2
            for r in range(wide):
                piece = up[:, r * columns : (r + 1) * columns] * mask_ref[slot, r]
                ext_ref[slot, r] = piece.astype(ext_ref.dtype)
    for t in range(frames):
        y = tap_sum(from_ref(ext_ref), fk_ref, t, rows, columns)
        res = frame_rows(from_ref(ext_ref), t + 2, 1, rows)
        out = (res.astype(jnp.float32) + y).astype(o_ref.dtype)
        for r in range(rows):
            o_ref[t, :, r, :] = out[:, r * columns : (r + 1) * columns]


def body(
    features,
    first_kernel,
    first_bias,
    first_gain,
    second_kernel,
    latent_weight,
    decode_kernel,
    decode_bias,
    decode_gain,
    upsample_weight,
    final_kernel,
):
    frames, channels, rows, columns = features.shape
    z_count = latent_weight.shape[1]
    dims = dict(frames=frames, rows=rows, columns=columns)
    own = features.transpose(0, 2, 1, 3)
    top = own[:, -2:]
    bottom = own[:, :2]
    previous = shift(own, 1, 0)
    band = lax.axis_index("rows")
    bands = lax.axis_size("rows")
    row_ids = lax.broadcasted_iota(jnp.int32, (frames + 2, rows + 2), 1)
    frame_ids = lax.broadcasted_iota(jnp.int32, (frames + 2, rows + 2), 0)
    inside = ((row_ids > 0) | (band > 0)) & ((row_ids < rows + 1) | (band < bands - 1))
    inside = inside & ((frame_ids >= 2) | (lax.axis_index("tm") > 0))
    params = (
        merged_kernel(first_kernel),
        merged_kernel(second_kernel),
        merged_kernel(decode_kernel),
        merged_kernel(final_kernel),
        jnp.stack([first_bias, first_gain, decode_bias, decode_gain], 1),
        inside.astype(jnp.float32),
    )
    vmem = pl.BlockSpec(memory_space=pltpu.VMEM)
    smem = pl.BlockSpec(memory_space=pltpu.SMEM)
    k1, k2, dk, fk, vec, mask = params
    from_above = shift(top, 0, 1)
    from_below = shift(bottom, 0, -1)
    late = pl.pallas_call(
        functools.partial(late_gate_kernel, **dims),
        out_shape=jax.ShapeDtypeStruct((2, rows + 2, channels, columns), jnp.bfloat16),
        in_specs=[vmem] * 5 + [smem],
    )(from_above, own, from_below, k1, vec, mask)
    prev_top, prev_bottom, late, *params = lax.optimization_barrier(
        (previous[:, -2:], previous[:, :2], late, *params)
    )
    k1, k2, dk, fk, vec, mask = params
    pieces = [
        shift(prev_top, 0, 1),
        previous,
        shift(prev_bottom, 0, -1),
        from_above,
        own,
        from_below,
    ]
    latent, lat_top, lat_bottom = pl.pallas_call(
        functools.partial(encoder_kernel, **dims),
        out_shape=(
            jax.ShapeDtypeStruct((1, z_count, rows, columns), jnp.bfloat16),
            jax.ShapeDtypeStruct((1, z_count, 2, columns), jnp.bfloat16),
            jax.ShapeDtypeStruct((1, z_count, 2, columns), jnp.bfloat16),
        ),
        in_specs=[vmem] * 9 + [smem, vmem, vmem],
        scratch_shapes=[pltpu.VMEM((frames, rows + 2, channels, columns), jnp.bfloat16)],
    )(
        *pieces,
        late,
        k1,
        vec,
        mask,
        k2,
        latent_weight,
    )
    lat_rows = jnp.concatenate(
        [shift(lat_top, 0, 1), latent, shift(lat_bottom, 0, -1)], 2
    )
    lat_frames = [shift(lat_rows, 3, 0), shift(lat_rows, 2, 0), shift(lat_rows, 1, 0), lat_rows]
    rebuilt = pl.pallas_call(
        functools.partial(decode_kernel_body, **dims),
        out_shape=jax.ShapeDtypeStruct((frames, channels, rows, columns), jnp.bfloat16),
        in_specs=[vmem] * 7 + [smem, vmem],
        scratch_shapes=[pltpu.VMEM((frames + 2, rows + 2, channels, columns), jnp.bfloat16)],
    )(
        *lat_frames,
        dk,
        vec,
        upsample_weight,
        mask,
        fk,
    )
    return (latent, rebuilt)


def solution(mesh):
    return jax.shard_map(
        body,
        mesh=mesh,
        in_specs=(P("tm", None, "rows", None), P(), P(), P(), P(), P(), P(), P(), P(), P(), P()),
        out_specs=(P("tm", None, "rows", None), P("tm", None, "rows", None)),
        check_vma=False,
    )
```

```python
import functools

import jax
import jax.numpy as jnp
from jax import lax
from jax.experimental import pallas as pl
from jax.experimental.pallas import tpu as pltpu
from jax.sharding import PartitionSpec as P


def shift(x, dt, dr):
    nt = lax.axis_size("tm")
    nr = lax.axis_size("rows")
    if dt == 0:
        pairs = [(r, r + dr) for r in range(nr) if 0 <= r + dr < nr]
        return lax.ppermute(x, "rows", pairs)
    if dr == 0:
        pairs = [(t, t + dt) for t in range(nt) if 0 <= t + dt < nt]
        return lax.ppermute(x, "tm", pairs)
    pairs = [
        (t * nr + r, (t + dt) * nr + r + dr)
        for t in range(nt)
        for r in range(nr)
        if 0 <= t + dt < nt and 0 <= r + dr < nr
    ]
    return lax.ppermute(x, ("tm", "rows"), pairs)


def merged_kernel(kernel):
    o, c = kernel.shape[3], kernel.shape[4]
    return kernel.transpose(2, 3, 0, 1, 4).reshape(3 * o, 9 * c)


def frame_rows(get, t, r0, rows):
    return jnp.concatenate([get(t, r0 + r) for r in range(rows)], axis=1)


def from_ref(x_ref):
    return lambda t, r: x_ref[t, r]


def tiled(parts, frames_each, rows_top, rows_mid):
    def get(t, r):
        block = parts[t // frames_each]
        f = t % frames_each
        if r < rows_top:
            return block[0][f, r]
        if r < rows_top + rows_mid:
            return block[1][f, r - rows_top]
        return block[2][f, r - rows_top - rows_mid]

    return get


def tap_sum(get, k_ref, t, rows, columns, count=1):
    pieces = []
    for a in range(3):
        for b in range(3):
            pieces.append(
                jnp.concatenate([frame_rows(get, t + i + a, b, rows) for i in range(count)], axis=1)
            )
    stacked = jnp.concatenate(pieces, axis=0)
    acc = jnp.dot(k_ref[...], stacked, preferred_element_type=jnp.float32)
    out_channels = acc.shape[0] // 3
    width = count * rows * columns
    lane = lax.broadcasted_iota(jnp.int32, (out_channels, width), 1) % columns
    left = pltpu.roll(acc[:out_channels], 1, 1)
    right = pltpu.roll(acc[2 * out_channels :], width - 1, 1)
    left = jnp.where(lane == 0, 0.0, left)
    right = jnp.where(lane == columns - 1, 0.0, right)
    return left + acc[out_channels : 2 * out_channels] + right


def at_row(get, r):
    return lambda t, rr: get(t, rr + r)


def late_gate_kernel(
    tp_ref, own_ref, bt_ref, k1_ref, vec_ref, mask_ref, o_ref, *, frames, rows, columns
):
    wide = rows + 2
    span = wide * columns
    x = tiled([(tp_ref, own_ref, bt_ref)], frames, 2, rows)
    y = tap_sum(x, k1_ref, frames - 4, wide, columns, 2) + vec_ref[:, 0:1]
    scale = lax.rsqrt(jnp.mean(y * y, axis=0, keepdims=True) + 1e-06)
    z = y * scale * vec_ref[:, 1:2]
    g = z / (1.0 + jnp.exp(-z))
    for i in range(2):
        for r in range(wide):
            lo = i * span + r * columns
            piece = g[:, lo : lo + columns] * mask_ref[frames + i, r]
            o_ref[i, r] = piece.astype(o_ref.dtype)


def encoder_kernel(
    tc_ref, pv_ref, bc_ref, tp_ref, own_ref, bt_ref, late_ref,
    k1_ref, vec_ref, mask_ref, k2_ref, w_ref, o_ref, top_ref, bottom_ref, g_ref,
    *, frames, rows, columns
):
    wide = rows + 2
    bias = vec_ref[:, 0:1]
    gain = vec_ref[:, 1:2]
    x = tiled([(tc_ref, pv_ref, bc_ref), (tp_ref, own_ref, bt_ref)], frames, 2, rows)
    span = wide * columns
    for t in range(0, frames, 2):
        y = tap_sum(x, k1_ref, t, wide, columns, 2) + bias
        scale = lax.rsqrt(jnp.mean(y * y, axis=0, keepdims=True) + 1e-06)
        z = y * scale * gain
        g = z / (1.0 + jnp.exp(-z))
        for i in range(2):
            for r in range(wide):
                lo = i * span + r * columns
                piece = g[:, lo : lo + columns] * mask_ref[t + i, r]
                g_ref[t + i, r] = piece.astype(g_ref.dtype)
    gated = lambda t, r: g_ref[t, r] if t < frames else late_ref[t - frames, r]
    total = None
    width = rows * columns
    for t in range(0, frames, 2):
        y = tap_sum(gated, k2_ref, t, rows, columns, 2)
        for i in range(2):
            res = frame_rows(x, t + i + frames, 2, rows)
            hidden = (res.astype(jnp.float32) + y[:, i * width : (i + 1) * width]).astype(jnp.bfloat16)
            part = jnp.dot(w_ref[t + i], hidden, preferred_element_type=jnp.float32)
            total = part if total is None else total + part
    for r in range(rows):
        piece = total[:, r * columns : (r + 1) * columns].astype(o_ref.dtype)
        o_ref[0, :, r, :] = piece
        if r < 2:
            bottom_ref[0, :, r, :] = piece
        if r >= rows - 2:
            top_ref[0, :, r - rows + 2, :] = piece


def decode_kernel_body(
    l3_ref, l2_ref, l1_ref, l0_ref, dk_ref, vec_ref, up_ref, mask_ref, fk_ref, o_ref, ext_ref,
    *, frames, rows, columns
):
    wide = rows + 2
    bias = vec_ref[:, 2:3]
    gain = vec_ref[:, 3:4]
    lat_refs = (l3_ref, l2_ref, l1_ref, l0_ref)
    lat = lambda t, r: lat_refs[t][0, :, r, :]
    for f in range(2):
        y = tap_sum(lat, dk_ref, f, wide, columns) + bias
        scale = lax.rsqrt(jnp.mean(y * y, axis=0, keepdims=True) + 1e-06)
        z = y * scale * gain
        act = (z / (1.0 + jnp.exp(-z))).astype(jnp.bfloat16)
        first_j = frames - 2 if f == 0 else 0
        for j in range(first_j, frames):
            up = jnp.dot(up_ref[j], act, preferred_element_type=jnp.float32)
            slot = j - first_j if f == 0 else j + 2
            for r in range(wide):
                piece = up[:, r * columns : (r + 1) * columns] * mask_ref[slot, r]
                ext_ref[slot, r] = piece.astype(ext_ref.dtype)
    for t in range(frames):
        for r in range(rows):
            y = tap_sum(at_row(from_ref(ext_ref), r), fk_ref, t, 1, columns)
            res = ext_ref[t + 2, r + 1]
            o_ref[t, :, r, :] = (res.astype(jnp.float32) + y).astype(o_ref.dtype)


def body(
    features,
    first_kernel,
    first_bias,
    first_gain,
    second_kernel,
    latent_weight,
    decode_kernel,
    decode_bias,
    decode_gain,
    upsample_weight,
    final_kernel,
):
    frames, channels, rows, columns = features.shape
    z_count = latent_weight.shape[1]
    dims = dict(frames=frames, rows=rows, columns=columns)
    own = features.transpose(0, 2, 1, 3)
    top = own[:, -2:]
    bottom = own[:, :2]
    previous = shift(own, 1, 0)
    band = lax.axis_index("rows")
    bands = lax.axis_size("rows")
    row_ids = lax.broadcasted_iota(jnp.int32, (frames + 2, rows + 2), 1)
    frame_ids = lax.broadcasted_iota(jnp.int32, (frames + 2, rows + 2), 0)
    inside = ((row_ids > 0) | (band > 0)) & ((row_ids < rows + 1) | (band < bands - 1))
    inside = inside & ((frame_ids >= 2) | (lax.axis_index("tm") > 0))
    params = (
        merged_kernel(first_kernel),
        merged_kernel(second_kernel),
        merged_kernel(decode_kernel),
        merged_kernel(final_kernel),
        jnp.stack([first_bias, first_gain, decode_bias, decode_gain], 1),
        inside.astype(jnp.float32),
    )
    prev_top, prev_bottom, *params = lax.optimization_barrier(
        (previous[:, -2:], previous[:, :2], *params)
    )
    k1, k2, dk, fk, vec, mask = params
    pieces = [
        shift(prev_top, 0, 1),
        previous,
        shift(prev_bottom, 0, -1),
        shift(top, 0, 1),
        own,
        shift(bottom, 0, -1),
    ]
    vmem = pl.BlockSpec(memory_space=pltpu.VMEM)
    smem = pl.BlockSpec(memory_space=pltpu.SMEM)
    late = pl.pallas_call(
        functools.partial(late_gate_kernel, **dims),
        out_shape=jax.ShapeDtypeStruct((2, rows + 2, channels, columns), jnp.bfloat16),
        in_specs=[vmem] * 5 + [smem],
    )(pieces[3], own, pieces[5], k1, vec, mask)
    latent, lat_top, lat_bottom = pl.pallas_call(
        functools.partial(encoder_kernel, **dims),
        out_shape=(
            jax.ShapeDtypeStruct((1, z_count, rows, columns), jnp.bfloat16),
            jax.ShapeDtypeStruct((1, z_count, 2, columns), jnp.bfloat16),
            jax.ShapeDtypeStruct((1, z_count, 2, columns), jnp.bfloat16),
        ),
        in_specs=[vmem] * 9 + [smem, vmem, vmem],
        scratch_shapes=[pltpu.VMEM((frames, rows + 2, channels, columns), jnp.bfloat16)],
    )(
        *pieces,
        late,
        k1,
        vec,
        mask,
        k2,
        latent_weight,
    )
    lat_rows = jnp.concatenate(
        [shift(lat_top, 0, 1), latent, shift(lat_bottom, 0, -1)], 2
    )
    lat_frames = [shift(lat_rows, 3, 0), shift(lat_rows, 2, 0), shift(lat_rows, 1, 0), lat_rows]
    rebuilt = pl.pallas_call(
        functools.partial(decode_kernel_body, **dims),
        out_shape=jax.ShapeDtypeStruct((frames, channels, rows, columns), jnp.bfloat16),
        in_specs=[vmem] * 7 + [smem, vmem],
        scratch_shapes=[pltpu.VMEM((frames + 2, rows + 2, channels, columns), jnp.bfloat16)],
    )(
        *lat_frames,
        dk,
        vec,
        upsample_weight,
        mask,
        fk,
    )
    return (latent, rebuilt)


def solution(mesh):
    return jax.shard_map(
        body,
        mesh=mesh,
        in_specs=(P("tm", None, "rows", None), P(), P(), P(), P(), P(), P(), P(), P(), P(), P()),
        out_specs=(P("tm", None, "rows", None), P("tm", None, "rows", None)),
        check_vma=False,
    )
```

```python
import functools

import jax
import jax.numpy as jnp
from jax import lax
from jax.experimental import pallas as pl
from jax.experimental.pallas import tpu as pltpu
from jax.sharding import PartitionSpec as P


def shift(x, dt, dr):
    nt = lax.axis_size("tm")
    nr = lax.axis_size("rows")
    if dt == 0:
        pairs = [(r, r + dr) for r in range(nr) if 0 <= r + dr < nr]
        return lax.ppermute(x, "rows", pairs)
    if dr == 0:
        pairs = [(t, t + dt) for t in range(nt) if 0 <= t + dt < nt]
        return lax.ppermute(x, "tm", pairs)
    pairs = [
        (t * nr + r, (t + dt) * nr + r + dr)
        for t in range(nt)
        for r in range(nr)
        if 0 <= t + dt < nt and 0 <= r + dr < nr
    ]
    return lax.ppermute(x, ("tm", "rows"), pairs)


def merged_kernel(kernel):
    o, c = kernel.shape[3], kernel.shape[4]
    return kernel.transpose(2, 3, 0, 1, 4).reshape(3 * o, 9 * c)


def frame_rows(get, t, r0, rows):
    return jnp.concatenate([get(t, r0 + r) for r in range(rows)], axis=1)


def from_ref(x_ref):
    return lambda t, r: x_ref[t, r]


def tiled(parts, frames_each, rows_top, rows_mid):
    def get(t, r):
        block = parts[t // frames_each]
        f = t % frames_each
        if r < rows_top:
            return block[0][f, r]
        if r < rows_top + rows_mid:
            return block[1][f, r - rows_top]
        return block[2][f, r - rows_top - rows_mid]

    return get


def tap_sum(get, k_ref, t, rows, columns, count=1):
    pieces = []
    for a in range(3):
        for b in range(3):
            pieces.append(
                jnp.concatenate([frame_rows(get, t + i + a, b, rows) for i in range(count)], axis=1)
            )
    stacked = jnp.concatenate(pieces, axis=0)
    acc = jnp.dot(k_ref[...], stacked, preferred_element_type=jnp.float32)
    out_channels = acc.shape[0] // 3
    width = count * rows * columns
    lane = lax.broadcasted_iota(jnp.int32, (out_channels, width), 1) % columns
    left = pltpu.roll(acc[:out_channels], 1, 1)
    right = pltpu.roll(acc[2 * out_channels :], width - 1, 1)
    left = jnp.where(lane == 0, 0.0, left)
    right = jnp.where(lane == columns - 1, 0.0, right)
    return left + acc[out_channels : 2 * out_channels] + right


def late_gate_kernel(
    tp_ref, own_ref, bt_ref, k1_ref, vec_ref, mask_ref, o_ref, *, frames, rows, columns
):
    wide = rows + 2
    span = wide * columns
    x = tiled([(tp_ref, own_ref, bt_ref)], frames, 2, rows)
    y = tap_sum(x, k1_ref, frames - 4, wide, columns, 2) + vec_ref[:, 0:1]
    scale = lax.rsqrt(jnp.mean(y * y, axis=0, keepdims=True) + 1e-06)
    z = y * scale * vec_ref[:, 1:2]
    g = z / (1.0 + jnp.exp(-z))
    for i in range(2):
        for r in range(wide):
            lo = i * span + r * columns
            piece = g[:, lo : lo + columns] * mask_ref[frames + i, r]
            o_ref[i, r] = piece.astype(o_ref.dtype)


def encoder_kernel(
    tc_any, pv_any, bc_any, tp_any, own_any, bt_any, late_any,
    k1_ref, vec_ref, mask_ref, k2_ref, w_ref, o_ref, top_ref, bottom_ref, g_ref,
    tc_ref, pv_ref, bc_ref, tp_ref, own_ref, bt_ref, late_ref, sems,
    *, frames, rows, columns
):
    sources = (tc_any, pv_any, bc_any, tp_any, own_any, bt_any, late_any)
    targets = (tc_ref, pv_ref, bc_ref, tp_ref, own_ref, bt_ref, late_ref)
    copies = [pltpu.make_async_copy(a, b, sems.at[i]) for i, (a, b) in enumerate(zip(sources, targets))]
    for c in copies:
        c.start()
    wide = rows + 2
    bias = vec_ref[:, 0:1]
    gain = vec_ref[:, 1:2]
    x = tiled([(tc_ref, pv_ref, bc_ref), (tp_ref, own_ref, bt_ref)], frames, 2, rows)
    span = wide * columns
    for t in range(0, frames, 2):
        for c in copies[:3] if t == 0 else copies[3:6]:
            c.wait()
        y = tap_sum(x, k1_ref, t, wide, columns, 2) + bias
        scale = lax.rsqrt(jnp.mean(y * y, axis=0, keepdims=True) + 1e-06)
        z = y * scale * gain
        g = z / (1.0 + jnp.exp(-z))
        for i in range(2):
            for r in range(wide):
                lo = i * span + r * columns
                piece = g[:, lo : lo + columns] * mask_ref[t + i, r]
                g_ref[t + i, r] = piece.astype(g_ref.dtype)
    copies[6].wait()
    gated = lambda t, r: g_ref[t, r] if t < frames else late_ref[t - frames, r]
    total = None
    width = rows * columns
    for t in range(0, frames, 2):
        y = tap_sum(gated, k2_ref, t, rows, columns, 2)
        for i in range(2):
            res = frame_rows(x, t + i + frames, 2, rows)
            hidden = (res.astype(jnp.float32) + y[:, i * width : (i + 1) * width]).astype(jnp.bfloat16)
            part = jnp.dot(w_ref[t + i], hidden, preferred_element_type=jnp.float32)
            total = part if total is None else total + part
    for r in range(rows):
        piece = total[:, r * columns : (r + 1) * columns].astype(o_ref.dtype)
        o_ref[0, :, r, :] = piece
        if r < 2:
            bottom_ref[0, :, r, :] = piece
        if r >= rows - 2:
            top_ref[0, :, r - rows + 2, :] = piece


def decode_kernel_body(
    l3_ref, l2_ref, l1_ref, l0_ref, dk_ref, vec_ref, up_ref, mask_ref, fk_ref, o_ref, ext_ref,
    *, frames, rows, columns
):
    wide = rows + 2
    bias = vec_ref[:, 2:3]
    gain = vec_ref[:, 3:4]
    lat_refs = (l3_ref, l2_ref, l1_ref, l0_ref)
    lat = lambda t, r: lat_refs[t][0, :, r, :]
    for f in range(2):
        y = tap_sum(lat, dk_ref, f, wide, columns) + bias
        scale = lax.rsqrt(jnp.mean(y * y, axis=0, keepdims=True) + 1e-06)
        z = y * scale * gain
        act = (z / (1.0 + jnp.exp(-z))).astype(jnp.bfloat16)
        first_j = frames - 2 if f == 0 else 0
        for j in range(first_j, frames):
            up = jnp.dot(up_ref[j], act, preferred_element_type=jnp.float32)
            slot = j - first_j if f == 0 else j + 2
            for r in range(wide):
                piece = up[:, r * columns : (r + 1) * columns] * mask_ref[slot, r]
                ext_ref[slot, r] = piece.astype(ext_ref.dtype)
    for t in range(frames):
        y = tap_sum(from_ref(ext_ref), fk_ref, t, rows, columns)
        res = frame_rows(from_ref(ext_ref), t + 2, 1, rows)
        out = (res.astype(jnp.float32) + y).astype(o_ref.dtype)
        for r in range(rows):
            o_ref[t, :, r, :] = out[:, r * columns : (r + 1) * columns]


def body(
    features,
    first_kernel,
    first_bias,
    first_gain,
    second_kernel,
    latent_weight,
    decode_kernel,
    decode_bias,
    decode_gain,
    upsample_weight,
    final_kernel,
):
    frames, channels, rows, columns = features.shape
    z_count = latent_weight.shape[1]
    dims = dict(frames=frames, rows=rows, columns=columns)
    own = features.transpose(0, 2, 1, 3)
    top = own[:, -2:]
    bottom = own[:, :2]
    previous = shift(own, 1, 0)
    band = lax.axis_index("rows")
    bands = lax.axis_size("rows")
    row_ids = lax.broadcasted_iota(jnp.int32, (frames + 2, rows + 2), 1)
    frame_ids = lax.broadcasted_iota(jnp.int32, (frames + 2, rows + 2), 0)
    inside = ((row_ids > 0) | (band > 0)) & ((row_ids < rows + 1) | (band < bands - 1))
    inside = inside & ((frame_ids >= 2) | (lax.axis_index("tm") > 0))
    params = (
        merged_kernel(first_kernel),
        merged_kernel(second_kernel),
        merged_kernel(decode_kernel),
        merged_kernel(final_kernel),
        jnp.stack([first_bias, first_gain, decode_bias, decode_gain], 1),
        inside.astype(jnp.float32),
    )
    prev_top, prev_bottom, *params = lax.optimization_barrier(
        (previous[:, -2:], previous[:, :2], *params)
    )
    k1, k2, dk, fk, vec, mask = params
    pieces = [
        shift(prev_top, 0, 1),
        previous,
        shift(prev_bottom, 0, -1),
        shift(top, 0, 1),
        own,
        shift(bottom, 0, -1),
    ]
    vmem = pl.BlockSpec(memory_space=pltpu.VMEM)
    smem = pl.BlockSpec(memory_space=pltpu.SMEM)
    late = pl.pallas_call(
        functools.partial(late_gate_kernel, **dims),
        out_shape=jax.ShapeDtypeStruct((2, rows + 2, channels, columns), jnp.bfloat16),
        in_specs=[vmem] * 5 + [smem],
    )(pieces[3], own, pieces[5], k1, vec, mask)
    latent, lat_top, lat_bottom = pl.pallas_call(
        functools.partial(encoder_kernel, **dims),
        out_shape=(
            jax.ShapeDtypeStruct((1, z_count, rows, columns), jnp.bfloat16),
            jax.ShapeDtypeStruct((1, z_count, 2, columns), jnp.bfloat16),
            jax.ShapeDtypeStruct((1, z_count, 2, columns), jnp.bfloat16),
        ),
        in_specs=[pl.BlockSpec(memory_space=pl.ANY)] * 7 + [vmem, vmem, smem, vmem, vmem],
        scratch_shapes=[pltpu.VMEM((frames, rows + 2, channels, columns), jnp.bfloat16)]
        + [pltpu.VMEM(p.shape, p.dtype) for p in pieces]
        + [pltpu.VMEM(late.shape, late.dtype), pltpu.SemaphoreType.DMA((7,))],
    )(
        *pieces,
        late,
        k1,
        vec,
        mask,
        k2,
        latent_weight,
    )
    lat_rows = jnp.concatenate(
        [shift(lat_top, 0, 1), latent, shift(lat_bottom, 0, -1)], 2
    )
    lat_frames = [shift(lat_rows, 3, 0), shift(lat_rows, 2, 0), shift(lat_rows, 1, 0), lat_rows]
    rebuilt = pl.pallas_call(
        functools.partial(decode_kernel_body, **dims),
        out_shape=jax.ShapeDtypeStruct((frames, channels, rows, columns), jnp.bfloat16),
        in_specs=[vmem] * 7 + [smem, vmem],
        scratch_shapes=[pltpu.VMEM((frames + 2, rows + 2, channels, columns), jnp.bfloat16)],
    )(
        *lat_frames,
        dk,
        vec,
        upsample_weight,
        mask,
        fk,
    )
    return (latent, rebuilt)


def solution(mesh):
    return jax.shard_map(
        body,
        mesh=mesh,
        in_specs=(P("tm", None, "rows", None), P(), P(), P(), P(), P(), P(), P(), P(), P(), P()),
        out_specs=(P("tm", None, "rows", None), P("tm", None, "rows", None)),
        check_vma=False,
    )
```

```python
import functools

import jax
import jax.numpy as jnp
from jax import lax
from jax.experimental import pallas as pl
from jax.experimental.pallas import tpu as pltpu
from jax.sharding import PartitionSpec as P


def shift(x, dt, dr):
    nt = lax.axis_size("tm")
    nr = lax.axis_size("rows")
    if dt == 0:
        pairs = [(r, r + dr) for r in range(nr) if 0 <= r + dr < nr]
        return lax.ppermute(x, "rows", pairs)
    if dr == 0:
        pairs = [(t, t + dt) for t in range(nt) if 0 <= t + dt < nt]
        return lax.ppermute(x, "tm", pairs)
    pairs = [
        (t * nr + r, (t + dt) * nr + r + dr)
        for t in range(nt)
        for r in range(nr)
        if 0 <= t + dt < nt and 0 <= r + dr < nr
    ]
    return lax.ppermute(x, ("tm", "rows"), pairs)


def merged_kernel(kernel):
    o, c = kernel.shape[3], kernel.shape[4]
    return kernel.transpose(2, 3, 0, 1, 4).reshape(3 * o, 9 * c)


def frame_rows(get, t, r0, rows):
    return jnp.concatenate([get(t, r0 + r) for r in range(rows)], axis=1)


def from_ref(x_ref):
    return lambda t, r: x_ref[t, r]


def tiled(parts, frames_each, rows_top, rows_mid):
    def get(t, r):
        block = parts[t // frames_each]
        f = t % frames_each
        if r < rows_top:
            return block[0][f, r]
        if r < rows_top + rows_mid:
            return block[1][f, r - rows_top]
        return block[2][f, r - rows_top - rows_mid]

    return get


def tap_sum(get, k_ref, t, rows, columns, count=1):
    pieces = []
    for a in range(3):
        for b in range(3):
            pieces.append(
                jnp.concatenate([frame_rows(get, t + i + a, b, rows) for i in range(count)], axis=1)
            )
    stacked = jnp.concatenate(pieces, axis=0)
    acc = jnp.dot(k_ref[...], stacked, preferred_element_type=jnp.float32)
    out_channels = acc.shape[0] // 3
    width = count * rows * columns
    lane = lax.broadcasted_iota(jnp.int32, (out_channels, width), 1) % columns
    left = pltpu.roll(acc[:out_channels], 1, 1)
    right = pltpu.roll(acc[2 * out_channels :], width - 1, 1)
    left = jnp.where(lane == 0, 0.0, left)
    right = jnp.where(lane == columns - 1, 0.0, right)
    return left + acc[out_channels : 2 * out_channels] + right


def late_gate_kernel(
    tp_ref, own_ref, bt_ref, k1_ref, vec_ref, mask_ref, o_ref, *, frames, rows, columns
):
    wide = rows + 2
    span = wide * columns
    x = tiled([(tp_ref, own_ref, bt_ref)], frames, 2, rows)
    y = tap_sum(x, k1_ref, frames - 4, wide, columns, 2) + vec_ref[:, 0:1]
    scale = lax.rsqrt(jnp.mean(y * y, axis=0, keepdims=True) + 1e-06)
    z = y * scale * vec_ref[:, 1:2]
    g = z / (1.0 + jnp.exp(-z))
    for i in range(2):
        for r in range(wide):
            lo = i * span + r * columns
            piece = g[:, lo : lo + columns] * mask_ref[frames + i, r]
            o_ref[i, r] = piece.astype(o_ref.dtype)


def encoder_kernel(
    tc_ref, pv_ref, bc_ref, tp_ref, own_ref, bt_ref, late_ref,
    k1_ref, vec_ref, mask_ref, k2_ref, w_ref, o_ref, top_ref, bottom_ref, g_ref,
    *, frames, rows, columns
):
    wide = rows + 2
    bias = vec_ref[:, 0:1]
    gain = vec_ref[:, 1:2]
    x = tiled([(tc_ref, pv_ref, bc_ref), (tp_ref, own_ref, bt_ref)], frames, 2, rows)
    span = wide * columns
    for t in range(0, frames, 2):
        y = tap_sum(x, k1_ref, t, wide, columns, 2) + bias
        scale = lax.rsqrt(jnp.mean(y * y, axis=0, keepdims=True) + 1e-06)
        z = y * scale * gain
        g = z / (1.0 + jnp.exp(-z))
        for i in range(2):
            for r in range(wide):
                lo = i * span + r * columns
                piece = g[:, lo : lo + columns] * mask_ref[t + i, r]
                g_ref[t + i, r] = piece.astype(g_ref.dtype)
    gated = lambda t, r: g_ref[t, r] if t < frames else late_ref[t - frames, r]
    total = None
    width = rows * columns
    for t in range(0, frames, 2):
        y = tap_sum(gated, k2_ref, t, rows, columns, 2)
        for i in range(2):
            res = frame_rows(x, t + i + frames, 2, rows)
            hidden = (res.astype(jnp.float32) + y[:, i * width : (i + 1) * width]).astype(jnp.bfloat16)
            part = jnp.dot(w_ref[t + i], hidden, preferred_element_type=jnp.float32)
            total = part if total is None else total + part
    for r in range(rows):
        piece = total[:, r * columns : (r + 1) * columns].astype(o_ref.dtype)
        o_ref[0, :, r, :] = piece
        if r < 2:
            bottom_ref[0, :, r, :] = piece
        if r >= rows - 2:
            top_ref[0, :, r - rows + 2, :] = piece


def decode_kernel_body(
    l3_ref, l2_ref, l1_ref, l0_ref, dk_ref, vec_ref, up_ref, mask_ref, fk_ref, o_ref, ext_ref,
    *, frames, rows, columns
):
    wide = rows + 2
    bias = vec_ref[:, 2:3]
    gain = vec_ref[:, 3:4]
    lat_refs = (l3_ref, l2_ref, l1_ref, l0_ref)
    lat = lambda t, r: lat_refs[t][0, :, r, :]
    both = tap_sum(lat, dk_ref, 0, wide, columns, 2) + bias
    scale = lax.rsqrt(jnp.mean(both * both, axis=0, keepdims=True) + 1e-06)
    z = both * scale * gain
    acts = (z / (1.0 + jnp.exp(-z))).astype(jnp.bfloat16)
    span = wide * columns
    for f in range(2):
        act = acts[:, f * span : (f + 1) * span]
        first_j = frames - 2 if f == 0 else 0
        for j in range(first_j, frames):
            up = jnp.dot(up_ref[j], act, preferred_element_type=jnp.float32)
            slot = j - first_j if f == 0 else j + 2
            for r in range(wide):
                piece = up[:, r * columns : (r + 1) * columns] * mask_ref[slot, r]
                ext_ref[slot, r] = piece.astype(ext_ref.dtype)
    for t in range(frames):
        y = tap_sum(from_ref(ext_ref), fk_ref, t, rows, columns)
        res = frame_rows(from_ref(ext_ref), t + 2, 1, rows)
        out = (res.astype(jnp.float32) + y).astype(o_ref.dtype)
        for r in range(rows):
            o_ref[t, :, r, :] = out[:, r * columns : (r + 1) * columns]


def body(
    features,
    first_kernel,
    first_bias,
    first_gain,
    second_kernel,
    latent_weight,
    decode_kernel,
    decode_bias,
    decode_gain,
    upsample_weight,
    final_kernel,
):
    frames, channels, rows, columns = features.shape
    z_count = latent_weight.shape[1]
    dims = dict(frames=frames, rows=rows, columns=columns)
    own = features.transpose(0, 2, 1, 3)
    top = own[:, -2:]
    bottom = own[:, :2]
    previous = shift(own, 1, 0)
    band = lax.axis_index("rows")
    bands = lax.axis_size("rows")
    row_ids = lax.broadcasted_iota(jnp.int32, (frames + 2, rows + 2), 1)
    frame_ids = lax.broadcasted_iota(jnp.int32, (frames + 2, rows + 2), 0)
    inside = ((row_ids > 0) | (band > 0)) & ((row_ids < rows + 1) | (band < bands - 1))
    inside = inside & ((frame_ids >= 2) | (lax.axis_index("tm") > 0))
    params = (
        merged_kernel(first_kernel),
        merged_kernel(second_kernel),
        merged_kernel(decode_kernel),
        merged_kernel(final_kernel),
        jnp.stack([first_bias, first_gain, decode_bias, decode_gain], 1),
        inside.astype(jnp.float32),
    )
    prev_top, prev_bottom, *params = lax.optimization_barrier(
        (previous[:, -2:], previous[:, :2], *params)
    )
    k1, k2, dk, fk, vec, mask = params
    pieces = [
        shift(prev_top, 0, 1),
        previous,
        shift(prev_bottom, 0, -1),
        shift(top, 0, 1),
        own,
        shift(bottom, 0, -1),
    ]
    vmem = pl.BlockSpec(memory_space=pltpu.VMEM)
    smem = pl.BlockSpec(memory_space=pltpu.SMEM)
    late = pl.pallas_call(
        functools.partial(late_gate_kernel, **dims),
        out_shape=jax.ShapeDtypeStruct((2, rows + 2, channels, columns), jnp.bfloat16),
        in_specs=[vmem] * 5 + [smem],
    )(pieces[3], own, pieces[5], k1, vec, mask)
    latent, lat_top, lat_bottom = pl.pallas_call(
        functools.partial(encoder_kernel, **dims),
        out_shape=(
            jax.ShapeDtypeStruct((1, z_count, rows, columns), jnp.bfloat16),
            jax.ShapeDtypeStruct((1, z_count, 2, columns), jnp.bfloat16),
            jax.ShapeDtypeStruct((1, z_count, 2, columns), jnp.bfloat16),
        ),
        in_specs=[vmem] * 9 + [smem, vmem, vmem],
        scratch_shapes=[pltpu.VMEM((frames, rows + 2, channels, columns), jnp.bfloat16)],
    )(
        *pieces,
        late,
        k1,
        vec,
        mask,
        k2,
        latent_weight,
    )
    lat_rows = jnp.concatenate(
        [shift(lat_top, 0, 1), latent, shift(lat_bottom, 0, -1)], 2
    )
    lat_frames = [shift(lat_rows, 3, 0), shift(lat_rows, 2, 0), shift(lat_rows, 1, 0), lat_rows]
    rebuilt = pl.pallas_call(
        functools.partial(decode_kernel_body, **dims),
        out_shape=jax.ShapeDtypeStruct((frames, channels, rows, columns), jnp.bfloat16),
        in_specs=[vmem] * 7 + [smem, vmem],
        scratch_shapes=[pltpu.VMEM((frames + 2, rows + 2, channels, columns), jnp.bfloat16)],
    )(
        *lat_frames,
        dk,
        vec,
        upsample_weight,
        mask,
        fk,
    )
    return (latent, rebuilt)


def solution(mesh):
    return jax.shard_map(
        body,
        mesh=mesh,
        in_specs=(P("tm", None, "rows", None), P(), P(), P(), P(), P(), P(), P(), P(), P(), P()),
        out_specs=(P("tm", None, "rows", None), P("tm", None, "rows", None)),
        check_vma=False,
    )
```

```python
import functools

import jax
import jax.numpy as jnp
from jax import lax
from jax.experimental import pallas as pl
from jax.experimental.pallas import tpu as pltpu
from jax.sharding import PartitionSpec as P


def shift(x, dt, dr):
    nt = lax.axis_size("tm")
    nr = lax.axis_size("rows")
    if dt == 0:
        pairs = [(r, r + dr) for r in range(nr) if 0 <= r + dr < nr]
        return lax.ppermute(x, "rows", pairs)
    if dr == 0:
        pairs = [(t, t + dt) for t in range(nt) if 0 <= t + dt < nt]
        return lax.ppermute(x, "tm", pairs)
    pairs = [
        (t * nr + r, (t + dt) * nr + r + dr)
        for t in range(nt)
        for r in range(nr)
        if 0 <= t + dt < nt and 0 <= r + dr < nr
    ]
    return lax.ppermute(x, ("tm", "rows"), pairs)


def merged_kernel(kernel):
    o, c = kernel.shape[3], kernel.shape[4]
    return kernel.transpose(2, 3, 0, 1, 4).reshape(3 * o, 9 * c)


def frame_rows(get, t, r0, rows):
    return jnp.concatenate([get(t, r0 + r) for r in range(rows)], axis=1)


def from_ref(x_ref):
    return lambda t, r: x_ref[t, r]


def tiled(parts, frames_each, rows_top, rows_mid):
    def get(t, r):
        block = parts[t // frames_each]
        f = t % frames_each
        if r < rows_top:
            return block[0][f, r]
        if r < rows_top + rows_mid:
            return block[1][f, r - rows_top]
        return block[2][f, r - rows_top - rows_mid]

    return get


def tap_sum(get, k_ref, t, rows, columns, count=1):
    pieces = []
    for a in range(3):
        for b in range(3):
            pieces.append(
                jnp.concatenate([frame_rows(get, t + i + a, b, rows) for i in range(count)], axis=1)
            )
    stacked = jnp.concatenate(pieces, axis=0)
    acc = jnp.dot(k_ref[...], stacked, preferred_element_type=jnp.float32)
    out_channels = acc.shape[0] // 3
    width = count * rows * columns
    lane = lax.broadcasted_iota(jnp.int32, (out_channels, width), 1) % columns
    left = pltpu.roll(acc[:out_channels], 1, 1)
    right = pltpu.roll(acc[2 * out_channels :], width - 1, 1)
    left = jnp.where(lane == 0, 0.0, left)
    right = jnp.where(lane == columns - 1, 0.0, right)
    return left + acc[out_channels : 2 * out_channels] + right


def late_gate_kernel(
    tp_ref, own_ref, bt_ref, k1_ref, vec_ref, mask_ref, o_ref, *, frames, rows, columns
):
    wide = rows + 2
    span = wide * columns
    x = tiled([(tp_ref, own_ref, bt_ref)], frames, 2, rows)
    y = tap_sum(x, k1_ref, frames - 4, wide, columns, 2) + vec_ref[:, 0:1]
    scale = lax.rsqrt(jnp.mean(y * y, axis=0, keepdims=True) + 1e-06)
    z = y * scale * vec_ref[:, 1:2]
    g = z / (1.0 + jnp.exp(-z))
    for i in range(2):
        for r in range(wide):
            lo = i * span + r * columns
            piece = g[:, lo : lo + columns] * mask_ref[frames + i, r]
            o_ref[i, r] = piece.astype(o_ref.dtype)


def encoder_kernel(
    tc_ref, pv_ref, bc_ref, tp_ref, own_ref, bt_ref, late_ref,
    k1_ref, vec_ref, mask_ref, k2_ref, w_ref, o_ref, top_ref, bottom_ref, g_ref,
    *, frames, rows, columns
):
    wide = rows + 2
    bias = vec_ref[:, 0:1]
    gain = vec_ref[:, 1:2]
    x = tiled([(tc_ref, pv_ref, bc_ref), (tp_ref, own_ref, bt_ref)], frames, 2, rows)
    span = wide * columns
    for t in range(0, frames, 2):
        y = tap_sum(x, k1_ref, t, wide, columns, 2) + bias
        scale = lax.rsqrt(jnp.mean(y * y, axis=0, keepdims=True) + 1e-06)
        z = y * scale * gain
        g = z / (1.0 + jnp.exp(-z))
        for i in range(2):
            for r in range(wide):
                lo = i * span + r * columns
                piece = g[:, lo : lo + columns] * mask_ref[t + i, r]
                g_ref[t + i, r] = piece.astype(g_ref.dtype)
    gated = lambda t, r: g_ref[t, r] if t < frames else late_ref[t - frames, r]
    total = None
    width = rows * columns
    for t in range(0, frames, 2):
        y = tap_sum(gated, k2_ref, t, rows, columns, 2)
        for i in range(2):
            res = frame_rows(x, t + i + frames, 2, rows)
            hidden = (res.astype(jnp.float32) + y[:, i * width : (i + 1) * width]).astype(jnp.bfloat16)
            part = jnp.dot(w_ref[t + i], hidden, preferred_element_type=jnp.float32)
            total = part if total is None else total + part
    for r in range(rows):
        piece = total[:, r * columns : (r + 1) * columns].astype(o_ref.dtype)
        o_ref[0, :, r, :] = piece
        if r < 2:
            bottom_ref[0, :, r, :] = piece
        if r >= rows - 2:
            top_ref[0, :, r - rows + 2, :] = piece


def decode_kernel_body(
    l3_ref, l2_ref, l1_ref, l0_ref, dk_ref, vec_ref, up_ref, mask_ref, fk_ref, o_ref, ext_ref,
    *, frames, rows, columns
):
    wide = rows + 2
    bias = vec_ref[:, 2:3]
    gain = vec_ref[:, 3:4]
    lat_refs = (l3_ref, l2_ref, l1_ref, l0_ref)
    lat = lambda t, r: lat_refs[t][0, :, r, :]
    both = tap_sum(lat, dk_ref, 0, wide, columns, 2) + bias
    scale = lax.rsqrt(jnp.mean(both * both, axis=0, keepdims=True) + 1e-06)
    z = both * scale * gain
    acts = (z / (1.0 + jnp.exp(-z))).astype(jnp.bfloat16)
    span = wide * columns
    for f in range(2):
        act = acts[:, f * span : (f + 1) * span]
        first_j = frames - 2 if f == 0 else 0
        for j in range(first_j, frames):
            up = jnp.dot(up_ref[j], act, preferred_element_type=jnp.float32)
            slot = j - first_j if f == 0 else j + 2
            for r in range(wide):
                piece = up[:, r * columns : (r + 1) * columns] * mask_ref[slot, r]
                ext_ref[slot, r] = piece.astype(ext_ref.dtype)
    width = rows * columns
    for t in range(0, frames, 2):
        y = tap_sum(from_ref(ext_ref), fk_ref, t, rows, columns, 2)
        for i in range(2):
            res = frame_rows(from_ref(ext_ref), t + i + 2, 1, rows)
            out = (res.astype(jnp.float32) + y[:, i * width : (i + 1) * width]).astype(o_ref.dtype)
            for r in range(rows):
                o_ref[t + i, :, r, :] = out[:, r * columns : (r + 1) * columns]


def body(
    features,
    first_kernel,
    first_bias,
    first_gain,
    second_kernel,
    latent_weight,
    decode_kernel,
    decode_bias,
    decode_gain,
    upsample_weight,
    final_kernel,
):
    frames, channels, rows, columns = features.shape
    z_count = latent_weight.shape[1]
    dims = dict(frames=frames, rows=rows, columns=columns)
    own = features.transpose(0, 2, 1, 3)
    top = own[:, -2:]
    bottom = own[:, :2]
    previous = shift(own, 1, 0)
    band = lax.axis_index("rows")
    bands = lax.axis_size("rows")
    row_ids = lax.broadcasted_iota(jnp.int32, (frames + 2, rows + 2), 1)
    frame_ids = lax.broadcasted_iota(jnp.int32, (frames + 2, rows + 2), 0)
    inside = ((row_ids > 0) | (band > 0)) & ((row_ids < rows + 1) | (band < bands - 1))
    inside = inside & ((frame_ids >= 2) | (lax.axis_index("tm") > 0))
    params = (
        merged_kernel(first_kernel),
        merged_kernel(second_kernel),
        merged_kernel(decode_kernel),
        merged_kernel(final_kernel),
        jnp.stack([first_bias, first_gain, decode_bias, decode_gain], 1),
        inside.astype(jnp.float32),
    )
    prev_top, prev_bottom, *params = lax.optimization_barrier(
        (previous[:, -2:], previous[:, :2], *params)
    )
    k1, k2, dk, fk, vec, mask = params
    pieces = [
        shift(prev_top, 0, 1),
        previous,
        shift(prev_bottom, 0, -1),
        shift(top, 0, 1),
        own,
        shift(bottom, 0, -1),
    ]
    vmem = pl.BlockSpec(memory_space=pltpu.VMEM)
    smem = pl.BlockSpec(memory_space=pltpu.SMEM)
    late = pl.pallas_call(
        functools.partial(late_gate_kernel, **dims),
        out_shape=jax.ShapeDtypeStruct((2, rows + 2, channels, columns), jnp.bfloat16),
        in_specs=[vmem] * 5 + [smem],
    )(pieces[3], own, pieces[5], k1, vec, mask)
    latent, lat_top, lat_bottom = pl.pallas_call(
        functools.partial(encoder_kernel, **dims),
        out_shape=(
            jax.ShapeDtypeStruct((1, z_count, rows, columns), jnp.bfloat16),
            jax.ShapeDtypeStruct((1, z_count, 2, columns), jnp.bfloat16),
            jax.ShapeDtypeStruct((1, z_count, 2, columns), jnp.bfloat16),
        ),
        in_specs=[vmem] * 9 + [smem, vmem, vmem],
        scratch_shapes=[pltpu.VMEM((frames, rows + 2, channels, columns), jnp.bfloat16)],
    )(
        *pieces,
        late,
        k1,
        vec,
        mask,
        k2,
        latent_weight,
    )
    lat_rows = jnp.concatenate(
        [shift(lat_top, 0, 1), latent, shift(lat_bottom, 0, -1)], 2
    )
    lat_frames = [shift(lat_rows, 3, 0), shift(lat_rows, 2, 0), shift(lat_rows, 1, 0), lat_rows]
    rebuilt = pl.pallas_call(
        functools.partial(decode_kernel_body, **dims),
        out_shape=jax.ShapeDtypeStruct((frames, channels, rows, columns), jnp.bfloat16),
        in_specs=[vmem] * 7 + [smem, vmem],
        scratch_shapes=[pltpu.VMEM((frames + 2, rows + 2, channels, columns), jnp.bfloat16)],
    )(
        *lat_frames,
        dk,
        vec,
        upsample_weight,
        mask,
        fk,
    )
    return (latent, rebuilt)


def solution(mesh):
    return jax.shard_map(
        body,
        mesh=mesh,
        in_specs=(P("tm", None, "rows", None), P(), P(), P(), P(), P(), P(), P(), P(), P(), P()),
        out_specs=(P("tm", None, "rows", None), P("tm", None, "rows", None)),
        check_vma=False,
    )
```
